256 devices in a mesh: grp: 4 (over x), tok: 8 (over z), mdl: 8 (over y, core).
Axes of the slice: x: 4, y: 4, z: 8, core: 2. Of those that a mesh axis runs over, the one named last changes fastest.
Arguments:
- hidden_in: bfloat16 [4, 1024, 5120], P('grp', 'tok', 'mdl'), may hold values from -8 to 8
- seg_ids: int32 [4, 1024], replicated, may hold values from 0 to 3, never falling along the last dimension, each value on 1 to 768 neighbouring positions
- request_prefix: int32 [4, 4], replicated, may hold values from 0 to 1
- page_table: int32 [32], replicated, may hold values from 0 to 31, each once
- prefix_cache: bfloat16 [32, 256, 8, 256], P(('grp', 'mdl'), None, 'tok'), may hold values from -200 to 200
- attn_gain: float32 [5120], P('mdl'), may hold values from 0.1 to 1.9
- w_query: bfloat16 [5120, 5120], P('mdl', 'tok'), may hold values from -0.078125 to 0.078125
- w_key: bfloat16 [5120, 1024], P('mdl', 'tok'), may hold values from -0.25 to 0.25
- w_value: bfloat16 [5120, 1024], P('mdl', 'tok'), may hold values from -0.078125 to 0.078125
- w_out: bfloat16 [5120, 5120], P('tok', 'mdl'), may hold values from -0.078125 to 0.078125
- ffn_gain: float32 [5120], P('mdl'), may hold values from 0.1 to 1.9
- w_gate: bfloat16 [5120, 14336], P('mdl', 'tok'), may hold values from -0.078125 to 0.078125
- w_up: bfloat16 [5120, 14336], P('mdl', 'tok'), may hold values from -0.078125 to 0.078125
- w_down: bfloat16 [14336, 5120], P('tok', 'mdl'), may hold values from -0.046875 to 0.046875
- final_gain: float32 [5120], replicated, may hold values from 0.1 to 1.9
- lm_head: bfloat16 [76800, 5120], P(('grp', 'tok', 'mdl')), may hold values from -0.25 to 0.25
Outputs:
- hidden_out: bfloat16 [4, 1024, 5120], P('grp', 'tok', 'mdl')
- new_kv: bfloat16 [4, 1024, 8, 256], P('grp', 'mdl', 'tok')
- req_norm: float32 [4, 4], P('grp')
- max_logit: float32 [4, 4], replicated
- logits: float32 [16, 76800], P(None, ('grp', 'tok', 'mdl'))
The draws below stay inside these ranges and needn't reach their ends.
Inputs may be any that keep to these rules, and one draw needn't show every extreme that they name: `seg_ids`: requests of a group are contiguous, in order, and none is empty. `page_table`: each physical slot holds exactly one logical page.
All inputs are finite; a program needn't handle non-finite values.
Results may differ from the reference program's by a relative error of at most 0.024.
Values may be sent and summed in bfloat16 or wider, within the bound.
No kernel may reach another device: no remote copies, remote signals or barrier semaphores. Data moves between devices by JAX's collectives and lax.ppermute only.
A program may use at most 128 MiB of HBM per device.

```python
import math
import jax
import jax.numpy as jnp
import numpy as np
from jax import lax

D = 5120
HEADS = 40
KVH = 8
HD = 128
FF = 14336
VOCAB = 76800
NPREFIX = 2
PREFIX = 4096
PAGE = 256
REQ = 4
SEQ = 1024
SLOTS = 32
N_GRP = 4
N_MDL = 8


def draw_hidden_in(key, part):
    full_shape = (N_GRP, SEQ, D)
    feature = jnp.arange(D, dtype=jnp.float32) / (D - 1)
    base_values = jnp.clip(jax.random.normal(key, full_shape, jnp.float32), -4.0, 4.0)
    scale_row = 0.6 * jnp.exp(feature * 1.0986123)
    return (base_values * scale_row[None, None, :]).astype(jnp.bfloat16)


def draw_prefix_cache(key, part):
    base_key = jax.random.fold_in(key, 0)
    full_shape = (SLOTS, PAGE, KVH, 2 * HD)
    base_values = jnp.clip(jax.random.normal(base_key, full_shape, jnp.float32), -6.0, 6.0)
    key_part = base_values[..., :HD] * 3.0
    value_part = base_values[..., HD:]
    return jnp.concatenate([key_part, value_part], -1).astype(jnp.bfloat16)


def plant(values, stream_key, least, largest):
    longest = values.shape.index(max(values.shape))
    spots = []
    for shift in (0, 1):
        where = [jax.random.randint(jax.random.fold_in(stream_key, axis), (), 0, length) for axis, length in enumerate(values.shape)]
        where[longest] = (where[longest] + shift) % values.shape[longest]
        spots.append(tuple(where))
    return values.at[spots[0]].set(least).at[spots[1]].set(largest)


def level_of(own_key, extent, cuts, low, top_value):
    factor_of, own = 1.0, jax.random.fold_in(own_key, 6)
    for dim, blocks in cuts:
        draws = jnp.exp(jax.random.uniform(jax.random.fold_in(own, dim), (blocks,), jnp.float32, low / len(cuts), top_value / len(cuts)))
        factor_of = factor_of * jnp.repeat(draws, extent[dim] // blocks).reshape([-1 if axis == dim else 1 for axis in range(len(extent))])
    return factor_of


def split_up(count, total, most, skew):
    loads = [(1 << 20) // math.isqrt(rank ** skew) + 1 for rank in range(2, count + 1)]
    surplus, given = total - most - (count - 1), [1] * (count - 1)
    while surplus > 0:
        free = [i for i in range(count - 1) if given[i] < most]
        pool, budget = sum([loads[i] for i in free]), surplus
        for i in free:
            more = min(most - given[i], max(1, budget * loads[i] // pool), surplus)
            given[i] = given[i] + more
            surplus = surplus - more
    return np.array([most] + given)


def uneven_parts(rng, number_of, total, limit, slope):
    if number_of == 2:
        one = jax.random.randint(rng, (), max(1, total - limit), min(limit, total - 1) + 1)
        return jnp.stack([one, total - one])
    tallies = jnp.asarray(split_up(number_of, total, limit, slope), jnp.int32)
    couples = (number_of - 1) // 2
    source_of, sink = tallies[1:1 + 2 * couples:2], tallies[2:2 + 2 * couples:2]
    margin = jnp.minimum(source_of - 1, limit - sink)
    shifted = jax.random.randint(jax.random.fold_in(rng, 1), (couples,), 0, 1 << 20) % (margin + 1)
    tallies = tallies.at[1:1 + 2 * couples:2].set(source_of - shifted).at[2:2 + 2 * couples:2].set(sink + shifted)
    return tallies[jax.random.permutation(jax.random.fold_in(rng, 2), number_of)]


def scatter_about(stream_key, extent, width, limit, cuts=(), kind=jnp.bfloat16):
    values = jax.random.normal(stream_key, extent, jnp.float32) * width
    if len(cuts) > 0:
        values = level_of(stream_key, extent, cuts, -0.22, 0.18) * values
    return jnp.clip(values, min=-limit, max=limit).astype(kind)


def setup_inputs(seed: int = 0) -> dict:
    key_of = jax.random.split(jax.random.key(seed), 17)
    return {
        "hidden_in": draw_hidden_in(jax.random.fold_in(key_of[16], 71), 0),
        "seg_ids": jax.vmap(lambda own: jnp.searchsorted(jnp.cumsum(uneven_parts(own, REQ, SEQ, SEQ * 3 // 4, 2)), jnp.arange(SEQ), side="right"))(jax.random.split(key_of[1], N_GRP)).reshape((N_GRP, SEQ)).astype(jnp.int32),
        "request_prefix": plant(jax.random.randint(key_of[2], (N_GRP, REQ), 0, NPREFIX), jax.random.fold_in(key_of[2], 1), 0, NPREFIX - 1).astype(jnp.int32),
        "page_table": jax.random.permutation(key_of[3], SLOTS).astype(jnp.int32),
        "prefix_cache": draw_prefix_cache(jax.random.fold_in(key_of[16], 71), 0),
        "attn_gain": jnp.clip(1.0 + 0.18 * jax.random.normal(key_of[5], (D,), jnp.float32), 0.1, 1.9),
        "w_query": scatter_about(key_of[6], (D, HEADS * HD), D ** -0.5, 0.078125, ((0, 8), (1, 8))),
        "w_key": scatter_about(key_of[7], (D, KVH * HD), (D // 9) ** -0.5, 0.25, ((0, 8), (1, 8))),
        "w_value": scatter_about(key_of[8], (D, KVH * HD), D ** -0.5, 0.078125, ((0, 8), (1, 8))),
        "w_out": scatter_about(key_of[9], (HEADS * HD, D), (HEADS * HD) ** -0.5, 0.078125, ((0, 8), (1, 8))),
        "ffn_gain": jnp.clip(1.0 + 0.18 * jax.random.normal(key_of[10], (D,), jnp.float32), 0.1, 1.9),
        "w_gate": scatter_about(key_of[11], (D, FF), D ** -0.5, 0.078125, ((0, 8), (1, 8))),
        "w_up": scatter_about(key_of[12], (D, FF), D ** -0.5, 0.078125, ((0, 8), (1, 8))),
        "w_down": scatter_about(key_of[13], (FF, D), FF ** -0.5, 0.046875, ((0, 8), (1, 8))),
        "final_gain": jnp.clip(1.0 + 0.18 * jax.random.normal(key_of[14], (D,), jnp.float32), 0.1, 1.9),
        "lm_head": scatter_about(key_of[15], (VOCAB, D), (D // 9) ** -0.5, 0.25, ((0, 256),)),
    }


EPS = 1e-06
THETA = 1000000.0
NEG = -1e+30

def rotate(tensor, positions):
    half_dim = tensor.shape[-1] // 2
    frequency = THETA ** (-(jnp.arange(half_dim, dtype=jnp.float32) * 2.0 / tensor.shape[-1]))
    angles = positions.astype(jnp.float32)[:, None] * frequency[None, :]
    cosine = jnp.cos(angles)[:, None, :]
    sine_part = jnp.sin(angles)[:, None, :]
    first_part = tensor[..., :half_dim]
    second = tensor[..., half_dim:]
    return jnp.concatenate([first_part * cosine - second * sine_part, second * cosine + first_part * sine_part], -1)

def group_layer(tokens, seg_row, prefix_row, slot_prefix, prefix_cache, attn_gain, w_query, w_key, w_value, w_out, ffn_gain, w_gate, w_up, w_down):
    group_size = HEADS // KVH
    score_scale = HD ** (-0.5)
    tok_f = tokens.astype(jnp.float32)
    normed = (tok_f * lax.rsqrt(lax.optimization_barrier(jnp.mean(tok_f * tok_f, -1, keepdims=True)) + EPS) * attn_gain).astype(jnp.bfloat16)
    queries = jnp.dot(normed, w_query, preferred_element_type=jnp.float32).reshape(SEQ, HEADS, HD)
    key_rows = jnp.dot(normed, w_key, preferred_element_type=jnp.float32).reshape(SEQ, KVH, HD)
    value_rows = jnp.dot(normed, w_value, preferred_element_type=jnp.float32).reshape(SEQ, KVH, HD)
    indices = jnp.arange(SEQ, dtype=jnp.int32)
    requests = jnp.arange(REQ, dtype=jnp.int32)
    member = seg_row[:, None] == requests[None, :]
    counts = lax.optimization_barrier(jnp.sum(member.astype(jnp.int32), 0))
    offsets = jnp.cumsum(counts) - counts
    positions = PREFIX + indices - offsets[seg_row]
    q_rot = rotate(queries, positions).astype(jnp.bfloat16)
    k_rot = rotate(key_rows, positions).astype(jnp.bfloat16)
    appended = jnp.concatenate([k_rot, value_rows.astype(jnp.bfloat16)], -1)
    row_prefix = prefix_row[seg_row]
    key_prefix = jnp.repeat(slot_prefix, PAGE)
    prefix_ok = (row_prefix[:, None] == key_prefix[None, :])[:, None, :]
    suffix_ok = ((seg_row[:, None] == seg_row[None, :]) & (indices[None, :] <= indices[:, None]))[:, None, :]

    def one_head(head_index):
        q_head = lax.dynamic_slice_in_dim(q_rot, head_index * group_size, group_size, 1).astype(jnp.float32)
        cache_head = lax.dynamic_index_in_dim(prefix_cache, head_index, 2, keepdims=False)
        cache_head = cache_head.reshape(SLOTS * PAGE, 2 * HD).astype(jnp.float32)
        suffix_head = lax.dynamic_index_in_dim(appended, head_index, 1, keepdims=False).astype(jnp.float32)
        pre_scores = jnp.einsum('sgd,kd->sgk', q_head, cache_head[:, :HD]) * score_scale
        suf_scores = jnp.einsum('sgd,td->sgt', q_head, suffix_head[:, :HD]) * score_scale
        pre_scores = jnp.where(prefix_ok, pre_scores, NEG)
        suf_scores = jnp.where(suffix_ok, suf_scores, NEG)
        row_max = jnp.maximum(lax.optimization_barrier(jnp.max(pre_scores, -1)), lax.optimization_barrier(jnp.max(suf_scores, -1)))
        pre_weights = jnp.where(prefix_ok, jnp.exp(pre_scores - row_max[..., None]), 0.0)
        suf_weights = jnp.where(suffix_ok, jnp.exp(suf_scores - row_max[..., None]), 0.0)
        row_total = lax.optimization_barrier(jnp.sum(pre_weights, -1)) + lax.optimization_barrier(jnp.sum(suf_weights, -1))
        pre_round = lax.optimization_barrier(pre_weights.astype(jnp.bfloat16)).astype(jnp.float32)
        suf_round = lax.optimization_barrier(suf_weights.astype(jnp.bfloat16)).astype(jnp.float32)
        mixed = jnp.einsum('sgk,kd->sgd', pre_round, cache_head[:, HD:]) + jnp.einsum('sgt,td->sgd', suf_round, suffix_head[:, HD:])
        return (mixed / row_total[..., None]).astype(jnp.bfloat16)
    heads_out = lax.map(one_head, jnp.arange(KVH, dtype=jnp.int32))
    attended = jnp.transpose(heads_out, (1, 0, 2, 3)).reshape(SEQ, HEADS * HD)
    residual = tok_f + jnp.dot(attended, w_out, preferred_element_type=jnp.float32)
    ffn_input = (residual * lax.rsqrt(lax.optimization_barrier(jnp.mean(residual * residual, -1, keepdims=True)) + EPS) * ffn_gain).astype(jnp.bfloat16)
    block_width = D // N_MDL
    gate = jnp.zeros((SEQ, FF), jnp.float32)
    up_sum = jnp.zeros((SEQ, FF), jnp.float32)
    for block in range(N_MDL):
        piece = ffn_input[:, block * block_width:(block + 1) * block_width]
        gate_part = jnp.dot(piece, w_gate[block * block_width:(block + 1) * block_width], preferred_element_type=jnp.float32)
        up_part = jnp.dot(piece, w_up[block * block_width:(block + 1) * block_width], preferred_element_type=jnp.float32)
        gate = gate + lax.optimization_barrier(gate_part.astype(jnp.bfloat16)).astype(jnp.float32)
        up_sum = up_sum + lax.optimization_barrier(up_part.astype(jnp.bfloat16)).astype(jnp.float32)
    hidden_units = (jax.nn.silu(gate) * up_sum).astype(jnp.bfloat16)
    final_rows = residual + jnp.dot(hidden_units, w_down, preferred_element_type=jnp.float32)
    row_squares = lax.optimization_barrier(jnp.sum(final_rows * final_rows, -1))
    req_squares = lax.optimization_barrier(jnp.sum(jnp.where(member, row_squares[:, None], 0.0), 0))
    req_norm = jnp.sqrt(req_squares / (counts.astype(jnp.float32) * D) + EPS)
    last_rows = final_rows[offsets + counts - 1]
    return (final_rows.astype(jnp.bfloat16), appended, req_norm, last_rows)

def reference(hidden_in, seg_ids, request_prefix, page_table, prefix_cache, attn_gain, w_query, w_key, w_value, w_out, ffn_gain, w_gate, w_up, w_down, final_gain, lm_head):
    pages_each = PREFIX // PAGE
    entries = jnp.arange(SLOTS, dtype=jnp.int32)
    slot_prefix = jnp.zeros((SLOTS,), jnp.int32).at[page_table].set(entries // pages_each)
    outputs = []
    appends = []
    norms = []
    lasts = []
    for group in range(hidden_in.shape[0]):
        result = group_layer(hidden_in[group], seg_ids[group], request_prefix[group], slot_prefix, prefix_cache, attn_gain, w_query, w_key, w_value, w_out, ffn_gain, w_gate, w_up, w_down)
        outputs.append(result[0])
        appends.append(result[1])
        norms.append(result[2])
        lasts.append(result[3])
    last_all = jnp.concatenate(lasts, 0)
    last_normed = (last_all * lax.rsqrt(lax.optimization_barrier(jnp.mean(last_all * last_all, -1, keepdims=True)) + EPS) * final_gain).astype(jnp.bfloat16)
    logits = lax.dot_general(last_normed, lm_head, (((1,), (1,)), ((), ())), preferred_element_type=jnp.float32)
    max_logit = lax.optimization_barrier(jnp.max(logits, -1)).reshape(hidden_in.shape[0], REQ)
    return (jnp.stack(outputs, 0), jnp.stack(appends, 0), jnp.stack(norms, 0), max_logit, logits)
```

```python
import jax
import jax.numpy as jnp
from jax import lax
from jax.sharding import PartitionSpec as P

PREFIX = 4096
PAGE = 256


EPS = 1e-06
THETA = 1000000.0
NEG = -1e30


def rotate(tensor, positions):
    half_dim = tensor.shape[-1] // 2
    frequency = THETA ** (-(jnp.arange(half_dim, dtype=jnp.float32) * 2.0 / tensor.shape[-1]))
    angles = positions.astype(jnp.float32)[:, None] * frequency[None, :]
    cosine = jnp.cos(angles)[:, None, :]
    sine_part = jnp.sin(angles)[:, None, :]
    first_part = tensor[..., :half_dim]
    second = tensor[..., half_dim:]
    return jnp.concatenate(
        [first_part * cosine - second * sine_part, second * cosine + first_part * sine_part], -1
    )


def on_device(
    hidden_in,
    seg_ids,
    request_prefix,
    page_table,
    prefix_cache,
    attn_gain,
    w_query,
    w_key,
    w_value,
    w_out,
    ffn_gain,
    w_gate,
    w_up,
    w_down,
    final_gain,
    lm_head,
):
    groups_total = seg_ids.shape[0]
    seq_len = seg_ids.shape[1]
    req_count = request_prefix.shape[1]
    tok_rows = hidden_in.shape[1]
    feat_dev = hidden_in.shape[2]
    model_width = feat_dev * lax.axis_size("mdl")
    head_dim = prefix_cache.shape[3] // 2
    kv_dev = prefix_cache.shape[2]
    heads_dev = w_query.shape[1] // head_dim
    group_size = heads_dev // kv_dev
    page_len = prefix_cache.shape[1]
    slot_total = page_table.shape[0]
    rows_mdl = seq_len // lax.axis_size("mdl")
    group_idx = lax.axis_index("grp")
    tok_idx = lax.axis_index("tok")
    mdl_idx = lax.axis_index("mdl")
    score_scale = head_dim ** (-0.5)
    tokens = hidden_in[0].astype(jnp.float32)
    squares = lax.psum(jnp.sum(tokens * tokens, -1), "mdl")
    normed = (tokens * lax.rsqrt(squares[:, None] / model_width + EPS) * attn_gain).astype(
        jnp.bfloat16
    )
    w_joined = jnp.concatenate([w_query, w_key, w_value], 1)
    partial_qkv = jnp.dot(
        lax.all_gather(normed, "tok", axis=0, tiled=True),
        w_joined,
        preferred_element_type=jnp.float32,
    )
    qkv_rows = lax.psum_scatter(partial_qkv, "mdl", scatter_dimension=0, tiled=True)
    q_cols = heads_dev * head_dim
    kv_cols = kv_dev * head_dim
    queries = qkv_rows[:, :q_cols].reshape(rows_mdl, heads_dev, head_dim)
    key_rows = qkv_rows[:, q_cols : q_cols + kv_cols].reshape(rows_mdl, kv_dev, head_dim)
    value_rows = qkv_rows[:, q_cols + kv_cols :].reshape(rows_mdl, kv_dev, head_dim)
    seg_row = lax.dynamic_index_in_dim(seg_ids, group_idx, 0, keepdims=False)
    prefix_row = lax.dynamic_index_in_dim(request_prefix, group_idx, 0, keepdims=False)
    requests = jnp.arange(req_count, dtype=jnp.int32)
    member = seg_row[:, None] == requests[None, :]
    counts = jnp.sum(member.astype(jnp.int32), 0)
    offsets = jnp.cumsum(counts) - counts
    row_start = mdl_idx * rows_mdl
    my_rows = row_start + jnp.arange(rows_mdl, dtype=jnp.int32)
    my_seg = lax.dynamic_slice_in_dim(seg_row, row_start, rows_mdl)
    my_member = my_seg[:, None] == requests[None, :]
    positions = PREFIX + my_rows - jnp.sum(jnp.where(my_member, offsets[None, :], 0), 1)
    my_prefix = jnp.sum(jnp.where(my_member, prefix_row[None, :], 0), 1)
    q_rot = (
        rotate(queries, positions)
        .astype(jnp.bfloat16)
        .reshape(rows_mdl, kv_dev, group_size, head_dim)
    )
    k_rot = rotate(key_rows, positions).astype(jnp.bfloat16)
    appended = jnp.concatenate([k_rot, value_rows.astype(jnp.bfloat16)], -1)
    suffix = lax.all_gather(appended, "mdl", axis=0, tiled=True)
    every_row = jnp.arange(seq_len, dtype=jnp.int32)
    suffix_ok = ((seg_row[None, :] == my_seg[:, None]) & (every_row[None, :] <= my_rows[:, None]))[
        :, None, None, :
    ]
    suffix_scores = (
        jnp.einsum(
            "rcgd,tcd->rcgt", q_rot, suffix[..., :head_dim], preferred_element_type=jnp.float32
        )
        * score_scale
    )
    suffix_scores = jnp.where(suffix_ok, suffix_scores, NEG)
    row_max = jnp.max(suffix_scores, -1)
    suffix_weights = jnp.where(suffix_ok, jnp.exp(suffix_scores - row_max[..., None]), 0.0)
    row_total = jnp.sum(suffix_weights, -1)
    mixed = jnp.einsum(
        "rcgt,tcd->rcgd",
        suffix_weights.astype(jnp.bfloat16),
        suffix[..., head_dim:],
        preferred_element_type=jnp.float32,
    )
    slot_ids = jnp.arange(slot_total, dtype=jnp.int32)
    pages_each = PREFIX // PAGE
    slot_prefix = jnp.sum(
        jnp.where(page_table[None, :] == slot_ids[:, None], (slot_ids // pages_each)[None, :], 0), 1
    )
    piece = lax.all_gather(prefix_cache, ("grp", "mdl"), axis=0, tiled=True)
    page_count = piece.shape[0]
    key_prefix = jnp.repeat(slot_prefix, page_len)
    allowed = (my_prefix[:, None] == key_prefix[None, :])[:, None, None, :]
    flat_pages = piece.reshape(page_count * page_len, kv_dev, 2 * head_dim)
    scores = (
        jnp.einsum(
            "rcgd,kcd->rcgk", q_rot, flat_pages[..., :head_dim], preferred_element_type=jnp.float32
        )
        * score_scale
    )
    scores = jnp.where(allowed, scores, NEG)
    new_max = jnp.maximum(row_max, jnp.max(scores, -1))
    factor = jnp.exp(row_max - new_max)
    page_weights = jnp.where(allowed, jnp.exp(scores - new_max[..., None]), 0.0)
    new_total = row_total * factor + jnp.sum(page_weights, -1)
    new_mixed = mixed * factor[..., None] + jnp.einsum(
        "rcgk,kcd->rcgd",
        page_weights.astype(jnp.bfloat16),
        flat_pages[..., head_dim:],
        preferred_element_type=jnp.float32,
    )
    attended = (
        (new_mixed / new_total[..., None])
        .astype(jnp.bfloat16)
        .reshape(rows_mdl, heads_dev * head_dim)
    )
    partial_out = jnp.dot(
        lax.all_gather(attended, "mdl", axis=0, tiled=True),
        w_out,
        preferred_element_type=jnp.float32,
    )
    residual = tokens + lax.psum_scatter(
        partial_out.astype(jnp.bfloat16), "tok", scatter_dimension=0, tiled=True
    ).astype(jnp.float32)
    squares_ffn = lax.psum(jnp.sum(residual * residual, -1), "mdl")
    ffn_input = (residual * lax.rsqrt(squares_ffn[:, None] / model_width + EPS) * ffn_gain).astype(
        jnp.bfloat16
    )
    w_pair = jnp.concatenate([w_gate, w_up], 1)
    ff_dev = w_gate.shape[1]
    partial_ffn = jnp.dot(
        lax.all_gather(ffn_input, "tok", axis=0, tiled=True),
        w_pair,
        preferred_element_type=jnp.float32,
    )
    summed = lax.psum_scatter(
        partial_ffn.astype(jnp.bfloat16), "mdl", scatter_dimension=0, tiled=True
    ).astype(jnp.float32)
    activated = (jax.nn.silu(summed[:, :ff_dev]) * summed[:, ff_dev:]).astype(jnp.bfloat16)
    partial_down = jnp.dot(
        lax.all_gather(activated, "mdl", axis=0, tiled=True),
        w_down,
        preferred_element_type=jnp.float32,
    )
    final_rows = residual + lax.psum_scatter(
        partial_down.astype(jnp.bfloat16), "tok", scatter_dimension=0, tiled=True
    ).astype(jnp.float32)
    tok_start = tok_idx * tok_rows
    my_tok_rows = tok_start + jnp.arange(tok_rows, dtype=jnp.int32)
    tok_seg = lax.dynamic_slice_in_dim(seg_row, tok_start, tok_rows)
    row_squares = jnp.sum(final_rows * final_rows, -1)
    req_squares = jnp.sum(
        jnp.where(tok_seg[:, None] == requests[None, :], row_squares[:, None], 0.0), 0
    )
    ends = offsets + counts - 1
    picked = ends[:, None] == my_tok_rows[None, :]
    last_part = jnp.sum(jnp.where(picked[:, :, None], final_rows[None, :, :], 0.0), 1)
    last_squares = jnp.sum(last_part * last_part, -1)
    packed = jnp.concatenate([last_part, req_squares[:, None], last_squares[:, None]], 1)
    packed = lax.psum(packed, "tok")
    blocks = lax.all_gather(packed, "mdl", axis=0, tiled=False)
    mdl_count = blocks.shape[0]
    last_rows = jnp.transpose(blocks[:, :, :feat_dev], (1, 0, 2)).reshape(req_count, model_width)
    req_total = jnp.sum(blocks[:, :, feat_dev], 0)
    last_total = jnp.sum(blocks[:, :, feat_dev + 1], 0)
    req_norm = jnp.sqrt(req_total / (counts.astype(jnp.float32) * model_width) + EPS)
    last_own = (
        last_rows * lax.rsqrt(last_total[:, None] / model_width + EPS) * final_gain
    ).astype(jnp.bfloat16)
    last_normed = lax.all_gather(last_own, "grp", axis=0, tiled=True)
    logits = lax.dot_general(
        last_normed, lm_head, (((1,), (1,)), ((), ())), preferred_element_type=jnp.float32
    )
    local_max = jnp.max(logits, -1)
    local_max = lax.pmax(local_max, "mdl")
    local_max = lax.pmax(local_max, "tok")
    max_logit = lax.pmax(local_max, "grp").reshape(groups_total, req_count)
    return (
        final_rows.astype(jnp.bfloat16)[None],
        appended[None],
        req_norm[None],
        max_logit,
        logits,
    )


def solution(mesh):
    return jax.shard_map(
        on_device,
        mesh=mesh,
        in_specs=(
            P("grp", "tok", "mdl"),
            P(),
            P(),
            P(),
            P(("grp", "mdl"), None, "tok", None),
            P("mdl"),
            P("mdl", "tok"),
            P("mdl", "tok"),
            P("mdl", "tok"),
            P("tok", "mdl"),
            P("mdl"),
            P("mdl", "tok"),
            P("mdl", "tok"),
            P("tok", "mdl"),
            P(),
            P(("grp", "tok", "mdl"), None),
        ),
        out_specs=(
            P("grp", "tok", "mdl"),
            P("grp", "mdl", "tok", None),
            P("grp", None),
            P(),
            P(None, ("grp", "tok", "mdl")),
        ),
        check_vma=False,
    )
```

```python
import jax
import jax.numpy as jnp
from jax import lax
from jax.sharding import PartitionSpec as P

PREFIX = 4096
PAGE = 256


EPS = 1e-06
THETA = 1000000.0
NEG = -1e30


def rotate(tensor, positions):
    half_dim = tensor.shape[-1] // 2
    frequency = THETA ** (-(jnp.arange(half_dim, dtype=jnp.float32) * 2.0 / tensor.shape[-1]))
    angles = positions.astype(jnp.float32)[:, None] * frequency[None, :]
    cosine = jnp.cos(angles)[:, None, :]
    sine_part = jnp.sin(angles)[:, None, :]
    first_part = tensor[..., :half_dim]
    second = tensor[..., half_dim:]
    return jnp.concatenate(
        [first_part * cosine - second * sine_part, second * cosine + first_part * sine_part], -1
    )


def scatter_sum(partial, axis):
    count = lax.axis_size(axis)
    pieces = partial.reshape((count, partial.shape[0] // count) + partial.shape[1:])
    pieces = lax.all_to_all(pieces, axis, 0, 0, tiled=False)
    return jnp.sum(pieces.astype(jnp.float32), 0)


def on_device(
    hidden_in,
    seg_ids,
    request_prefix,
    page_table,
    prefix_cache,
    attn_gain,
    w_query,
    w_key,
    w_value,
    w_out,
    ffn_gain,
    w_gate,
    w_up,
    w_down,
    final_gain,
    lm_head,
):
    groups_total = seg_ids.shape[0]
    seq_len = seg_ids.shape[1]
    req_count = request_prefix.shape[1]
    tok_rows = hidden_in.shape[1]
    feat_dev = hidden_in.shape[2]
    model_width = feat_dev * lax.axis_size("mdl")
    head_dim = prefix_cache.shape[3] // 2
    kv_dev = prefix_cache.shape[2]
    heads_dev = w_query.shape[1] // head_dim
    group_size = heads_dev // kv_dev
    page_len = prefix_cache.shape[1]
    slot_total = page_table.shape[0]
    rows_mdl = seq_len // lax.axis_size("mdl")
    group_idx = lax.axis_index("grp")
    tok_idx = lax.axis_index("tok")
    mdl_idx = lax.axis_index("mdl")
    score_scale = head_dim ** (-0.5)
    tokens = hidden_in[0].astype(jnp.float32)
    hidden_all = lax.all_gather(hidden_in[0], "tok", axis=0, tiled=True)
    squares = lax.psum(jnp.sum(tokens * tokens, -1), "mdl")
    squares_all = lax.all_gather(squares, "tok", axis=0, tiled=True)
    hidden_all_f = hidden_all.astype(jnp.float32)
    normed_all = (
        hidden_all_f * lax.rsqrt(squares_all[:, None] / model_width + EPS) * attn_gain
    ).astype(jnp.bfloat16)
    w_joined = jnp.concatenate([w_query, w_key, w_value], 1)
    partial_qkv = jnp.dot(normed_all, w_joined, preferred_element_type=jnp.float32)
    qkv_rows = lax.psum_scatter(partial_qkv, "mdl", scatter_dimension=0, tiled=True)
    q_cols = heads_dev * head_dim
    kv_cols = kv_dev * head_dim
    queries = qkv_rows[:, :q_cols].reshape(rows_mdl, heads_dev, head_dim)
    key_rows = qkv_rows[:, q_cols : q_cols + kv_cols].reshape(rows_mdl, kv_dev, head_dim)
    value_rows = qkv_rows[:, q_cols + kv_cols :].reshape(rows_mdl, kv_dev, head_dim)
    seg_row = lax.dynamic_index_in_dim(seg_ids, group_idx, 0, keepdims=False)
    prefix_row = lax.dynamic_index_in_dim(request_prefix, group_idx, 0, keepdims=False)
    requests = jnp.arange(req_count, dtype=jnp.int32)
    member = seg_row[:, None] == requests[None, :]
    counts = jnp.sum(member.astype(jnp.int32), 0)
    offsets = jnp.cumsum(counts) - counts
    row_start = mdl_idx * rows_mdl
    my_rows = row_start + jnp.arange(rows_mdl, dtype=jnp.int32)
    my_seg = lax.dynamic_slice_in_dim(seg_row, row_start, rows_mdl)
    my_member = my_seg[:, None] == requests[None, :]
    positions = PREFIX + my_rows - jnp.sum(jnp.where(my_member, offsets[None, :], 0), 1)
    my_prefix = jnp.sum(jnp.where(my_member, prefix_row[None, :], 0), 1)
    q_rot = (
        rotate(queries, positions)
        .astype(jnp.bfloat16)
        .reshape(rows_mdl, kv_dev, group_size, head_dim)
    )
    k_rot = rotate(key_rows, positions).astype(jnp.bfloat16)
    appended = jnp.concatenate([k_rot, value_rows.astype(jnp.bfloat16)], -1)
    suffix = lax.all_gather(appended, "mdl", axis=0, tiled=True)
    every_row = jnp.arange(seq_len, dtype=jnp.int32)
    suffix_ok = ((seg_row[None, :] == my_seg[:, None]) & (every_row[None, :] <= my_rows[:, None]))[
        :, None, None, :
    ]
    suffix_scores = (
        jnp.einsum(
            "rcgd,tcd->rcgt", q_rot, suffix[..., :head_dim], preferred_element_type=jnp.float32
        )
        * score_scale
    )
    suffix_scores = jnp.where(suffix_ok, suffix_scores, NEG)
    row_max = jnp.max(suffix_scores, -1)
    suffix_weights = jnp.where(suffix_ok, jnp.exp(suffix_scores - row_max[..., None]), 0.0)
    row_total = jnp.sum(suffix_weights, -1)
    mixed = jnp.einsum(
        "rcgt,tcd->rcgd",
        suffix_weights.astype(jnp.bfloat16),
        suffix[..., head_dim:],
        preferred_element_type=jnp.float32,
    )
    slot_ids = jnp.arange(slot_total, dtype=jnp.int32)
    pages_each = PREFIX // PAGE
    slot_prefix = jnp.sum(
        jnp.where(page_table[None, :] == slot_ids[:, None], (slot_ids // pages_each)[None, :], 0), 1
    )
    piece = lax.all_gather(prefix_cache, ("grp", "mdl"), axis=0, tiled=True)
    page_count = piece.shape[0]
    key_prefix = jnp.repeat(slot_prefix, page_len)
    allowed = (my_prefix[:, None] == key_prefix[None, :])[:, None, None, :]
    flat_pages = piece.reshape(page_count * page_len, kv_dev, 2 * head_dim)
    scores = (
        jnp.einsum(
            "rcgd,kcd->rcgk", q_rot, flat_pages[..., :head_dim], preferred_element_type=jnp.float32
        )
        * score_scale
    )
    scores = jnp.where(allowed, scores, NEG)
    new_max = jnp.maximum(row_max, jnp.max(scores, -1))
    factor = jnp.exp(row_max - new_max)
    page_weights = jnp.where(allowed, jnp.exp(scores - new_max[..., None]), 0.0)
    new_total = row_total * factor + jnp.sum(page_weights, -1)
    new_mixed = mixed * factor[..., None] + jnp.einsum(
        "rcgk,kcd->rcgd",
        page_weights.astype(jnp.bfloat16),
        flat_pages[..., head_dim:],
        preferred_element_type=jnp.float32,
    )
    attended = (
        (new_mixed / new_total[..., None])
        .astype(jnp.bfloat16)
        .reshape(rows_mdl, heads_dev * head_dim)
    )
    partial_out = jnp.dot(
        lax.all_gather(attended, "mdl", axis=0, tiled=True),
        w_out,
        preferred_element_type=jnp.float32,
    )
    out_sum = scatter_sum(partial_out.astype(jnp.bfloat16), "tok").astype(jnp.bfloat16)
    residual = tokens + out_sum.astype(jnp.float32)
    out_all = lax.all_gather(out_sum, "tok", axis=0, tiled=True)
    squares_ffn = lax.psum(jnp.sum(residual * residual, -1), "mdl")
    squares_ffn_all = lax.all_gather(squares_ffn, "tok", axis=0, tiled=True)
    residual_all = hidden_all_f + out_all.astype(jnp.float32)
    ffn_all = (
        residual_all * lax.rsqrt(squares_ffn_all[:, None] / model_width + EPS) * ffn_gain
    ).astype(jnp.bfloat16)
    w_pair = jnp.concatenate([w_gate, w_up], 1)
    ff_dev = w_gate.shape[1]
    partial_ffn = jnp.dot(ffn_all, w_pair, preferred_element_type=jnp.float32)
    summed = lax.psum_scatter(
        partial_ffn.astype(jnp.bfloat16), "mdl", scatter_dimension=0, tiled=True
    ).astype(jnp.float32)
    activated = (jax.nn.silu(summed[:, :ff_dev]) * summed[:, ff_dev:]).astype(jnp.bfloat16)
    partial_down = jnp.dot(
        lax.all_gather(activated, "mdl", axis=0, tiled=True),
        w_down,
        preferred_element_type=jnp.float32,
    )
    final_rows = residual + scatter_sum(partial_down.astype(jnp.bfloat16), "tok")
    tok_start = tok_idx * tok_rows
    my_tok_rows = tok_start + jnp.arange(tok_rows, dtype=jnp.int32)
    tok_seg = lax.dynamic_slice_in_dim(seg_row, tok_start, tok_rows)
    row_squares = jnp.sum(final_rows * final_rows, -1)
    req_squares = jnp.sum(
        jnp.where(tok_seg[:, None] == requests[None, :], row_squares[:, None], 0.0), 0
    )
    ends = offsets + counts - 1
    picked = ends[:, None] == my_tok_rows[None, :]
    last_part = jnp.sum(jnp.where(picked[:, :, None], final_rows[None, :, :], 0.0), 1)
    last_squares = jnp.sum(last_part * last_part, -1)
    packed = jnp.concatenate([last_part, req_squares[:, None], last_squares[:, None]], 1)
    packed = lax.psum(packed, "tok")
    blocks = lax.all_gather(packed, "mdl", axis=0, tiled=False)
    mdl_count = blocks.shape[0]
    last_rows = jnp.transpose(blocks[:, :, :feat_dev], (1, 0, 2)).reshape(req_count, model_width)
    req_total = jnp.sum(blocks[:, :, feat_dev], 0)
    last_total = jnp.sum(blocks[:, :, feat_dev + 1], 0)
    req_norm = jnp.sqrt(req_total / (counts.astype(jnp.float32) * model_width) + EPS)
    last_own = (
        last_rows * lax.rsqrt(last_total[:, None] / model_width + EPS) * final_gain
    ).astype(jnp.bfloat16)
    last_normed = lax.all_gather(last_own, "grp", axis=0, tiled=True)
    logits = lax.dot_general(
        last_normed, lm_head, (((1,), (1,)), ((), ())), preferred_element_type=jnp.float32
    )
    local_max = jnp.max(logits, -1)
    local_max = lax.pmax(local_max, "mdl")
    local_max = lax.pmax(local_max, "tok")
    max_logit = lax.pmax(local_max, "grp").reshape(groups_total, req_count)
    return (
        final_rows.astype(jnp.bfloat16)[None],
        appended[None],
        req_norm[None],
        max_logit,
        logits,
    )


def solution(mesh):
    return jax.shard_map(
        on_device,
        mesh=mesh,
        in_specs=(
            P("grp", "tok", "mdl"),
            P(),
            P(),
            P(),
            P(("grp", "mdl"), None, "tok", None),
            P("mdl"),
            P("mdl", "tok"),
            P("mdl", "tok"),
            P("mdl", "tok"),
            P("tok", "mdl"),
            P("mdl"),
            P("mdl", "tok"),
            P("mdl", "tok"),
            P("tok", "mdl"),
            P(),
            P(("grp", "tok", "mdl"), None),
        ),
        out_specs=(
            P("grp", "tok", "mdl"),
            P("grp", "mdl", "tok", None),
            P("grp", None),
            P(),
            P(None, ("grp", "tok", "mdl")),
        ),
        check_vma=False,
    )
```

```python
import functools

import jax
import jax.numpy as jnp
from jax import lax
from jax.sharding import PartitionSpec as P
from jax.experimental import pallas as pl

PREFIX = 4096
PAGE = 256


EPS = 1e-06
THETA = 1000000.0
NEG = -1e30
BK = 512


def attn_kernel(q_ref, pkv_ref, skv_ref, rp_ref, rs_ref, ri_ref, kp_ref, ks_ref, o_ref, *, scale, head_dim):
    q = q_ref[...]
    rows = q.shape[0]
    row_prefix = rp_ref[...]
    row_seg = rs_ref[...]
    row_idx = ri_ref[...]
    n_pre = pkv_ref.shape[0] // BK
    n_suf = skv_ref.shape[0] // BK

    def pre_block(b):
        start = pl.multiple_of(b * BK, BK)
        kv = pkv_ref[pl.ds(start, BK), :]
        s = lax.dot_general(q, kv[:, :head_dim], (((1,), (1,)), ((), ())), preferred_element_type=jnp.float32) * scale
        ok = row_prefix == kp_ref[:, pl.ds(start, BK)]
        return s, ok, kv[:, head_dim:]

    def suf_block(b):
        start = pl.multiple_of(b * BK, BK)
        kv = skv_ref[pl.ds(start, BK), :]
        s = lax.dot_general(q, kv[:, :head_dim], (((1,), (1,)), ((), ())), preferred_element_type=jnp.float32) * scale
        key_idx = start + lax.broadcasted_iota(jnp.int32, (1, BK), 1)
        ok = (row_seg == ks_ref[:, pl.ds(start, BK)]) & (key_idx <= row_idx)
        return s, ok, kv[:, head_dim:]

    def max_step(block):
        def step(b, m):
            s, ok, _ = block(b)
            return jnp.maximum(m, jnp.max(jnp.where(ok, s, NEG), -1, keepdims=True))
        return step

    m = jnp.full((rows, 1), NEG, jnp.float32)
    m = lax.fori_loop(0, n_pre, max_step(pre_block), m)
    m = lax.fori_loop(0, n_suf, max_step(suf_block), m)

    def sum_step(block):
        def step(b, carry):
            total, acc = carry
            s, ok, v = block(b)
            p = jnp.where(ok, jnp.exp(s - m), 0.0)
            total = total + jnp.sum(p, -1, keepdims=True)
            acc = acc + jnp.dot(p.astype(jnp.bfloat16), v, preferred_element_type=jnp.float32)
            return total, acc
        return step

    carry = (jnp.zeros((rows, 1), jnp.float32), jnp.zeros((rows, head_dim), jnp.float32))
    carry = lax.fori_loop(0, n_pre, sum_step(pre_block), carry)
    total, acc = lax.fori_loop(0, n_suf, sum_step(suf_block), carry)
    o_ref[...] = (acc / total).astype(o_ref.dtype)


def attention(q, pkv, skv, row_prefix, row_seg, row_idx, key_prefix, key_seg, *, scale, block_rows=128):
    n_rows, head_dim = q.shape
    kern = functools.partial(attn_kernel, scale=scale, head_dim=head_dim)
    full = lambda shape: pl.BlockSpec(shape, lambda i: (0, 0))
    rowb = lambda w: pl.BlockSpec((block_rows, w), lambda i: (i, 0))
    return pl.pallas_call(
        kern,
        grid=(n_rows // block_rows,),
        in_specs=[rowb(head_dim), full(pkv.shape), full(skv.shape), rowb(1), rowb(1), rowb(1), full(key_prefix.shape), full(key_seg.shape)],
        out_specs=rowb(head_dim),
        out_shape=jax.ShapeDtypeStruct((n_rows, head_dim), jnp.bfloat16),
    )(q, pkv, skv, row_prefix, row_seg, row_idx, key_prefix, key_seg)


def rotate(tensor, positions):
    half_dim = tensor.shape[-1] // 2
    frequency = THETA ** (-(jnp.arange(half_dim, dtype=jnp.float32) * 2.0 / tensor.shape[-1]))
    angles = positions.astype(jnp.float32)[:, None] * frequency[None, :]
    cosine = jnp.cos(angles)[:, None, :]
    sine_part = jnp.sin(angles)[:, None, :]
    first_part = tensor[..., :half_dim]
    second = tensor[..., half_dim:]
    return jnp.concatenate(
        [first_part * cosine - second * sine_part, second * cosine + first_part * sine_part], -1
    )


def scatter_sum(partial, axis):
    count = lax.axis_size(axis)
    pieces = partial.reshape((count, partial.shape[0] // count) + partial.shape[1:])
    pieces = lax.all_to_all(pieces, axis, 0, 0, tiled=False)
    return jnp.sum(pieces.astype(jnp.float32), 0)


def on_device(
    hidden_in,
    seg_ids,
    request_prefix,
    page_table,
    prefix_cache,
    attn_gain,
    w_query,
    w_key,
    w_value,
    w_out,
    ffn_gain,
    w_gate,
    w_up,
    w_down,
    final_gain,
    lm_head,
):
    groups_total = seg_ids.shape[0]
    seq_len = seg_ids.shape[1]
    req_count = request_prefix.shape[1]
    tok_rows = hidden_in.shape[1]
    feat_dev = hidden_in.shape[2]
    model_width = feat_dev * lax.axis_size("mdl")
    head_dim = prefix_cache.shape[3] // 2
    kv_dev = prefix_cache.shape[2]
    heads_dev = w_query.shape[1] // head_dim
    group_size = heads_dev // kv_dev
    page_len = prefix_cache.shape[1]
    slot_total = page_table.shape[0]
    rows_mdl = seq_len // lax.axis_size("mdl")
    group_idx = lax.axis_index("grp")
    tok_idx = lax.axis_index("tok")
    mdl_idx = lax.axis_index("mdl")
    score_scale = head_dim ** (-0.5)
    tokens = hidden_in[0].astype(jnp.float32)
    hidden_all = lax.all_gather(hidden_in[0], "tok", axis=0, tiled=True)
    squares = lax.psum(jnp.sum(tokens * tokens, -1), "mdl")
    squares_all = lax.all_gather(squares, "tok", axis=0, tiled=True)
    hidden_all_f = hidden_all.astype(jnp.float32)
    normed_all = (
        hidden_all_f * lax.rsqrt(squares_all[:, None] / model_width + EPS) * attn_gain
    ).astype(jnp.bfloat16)
    w_joined = jnp.concatenate([w_query, w_key, w_value], 1)
    partial_qkv = jnp.dot(normed_all, w_joined, preferred_element_type=jnp.float32)
    qkv_rows = lax.psum_scatter(partial_qkv, "mdl", scatter_dimension=0, tiled=True)
    q_cols = heads_dev * head_dim
    kv_cols = kv_dev * head_dim
    queries = qkv_rows[:, :q_cols].reshape(rows_mdl, heads_dev, head_dim)
    key_rows = qkv_rows[:, q_cols : q_cols + kv_cols].reshape(rows_mdl, kv_dev, head_dim)
    value_rows = qkv_rows[:, q_cols + kv_cols :].reshape(rows_mdl, kv_dev, head_dim)
    seg_row = lax.dynamic_index_in_dim(seg_ids, group_idx, 0, keepdims=False)
    prefix_row = lax.dynamic_index_in_dim(request_prefix, group_idx, 0, keepdims=False)
    requests = jnp.arange(req_count, dtype=jnp.int32)
    member = seg_row[:, None] == requests[None, :]
    counts = jnp.sum(member.astype(jnp.int32), 0)
    offsets = jnp.cumsum(counts) - counts
    row_start = mdl_idx * rows_mdl
    my_rows = row_start + jnp.arange(rows_mdl, dtype=jnp.int32)
    my_seg = lax.dynamic_slice_in_dim(seg_row, row_start, rows_mdl)
    my_member = my_seg[:, None] == requests[None, :]
    positions = PREFIX + my_rows - jnp.sum(jnp.where(my_member, offsets[None, :], 0), 1)
    my_prefix = jnp.sum(jnp.where(my_member, prefix_row[None, :], 0), 1)
    q_rot = (
        rotate(queries, positions)
        .astype(jnp.bfloat16)
        .reshape(rows_mdl, kv_dev, group_size, head_dim)
    )
    k_rot = rotate(key_rows, positions).astype(jnp.bfloat16)
    appended = jnp.concatenate([k_rot, value_rows.astype(jnp.bfloat16)], -1)
    suffix = lax.all_gather(appended, "mdl", axis=0, tiled=True)
    slot_ids = jnp.arange(slot_total, dtype=jnp.int32)
    pages_each = PREFIX // PAGE
    slot_prefix = jnp.sum(
        jnp.where(page_table[None, :] == slot_ids[:, None], (slot_ids // pages_each)[None, :], 0), 1
    )
    piece = lax.all_gather(prefix_cache, ("grp", "mdl"), axis=0, tiled=True)
    page_count = piece.shape[0]
    key_prefix = jnp.repeat(slot_prefix, page_len)[None, :]
    flat_pages = piece.reshape(page_count * page_len, 2 * head_dim)
    flat_suffix = suffix.reshape(seq_len, 2 * head_dim)
    row_prefix = jnp.repeat(my_prefix, group_size)[:, None]
    row_seg = jnp.repeat(my_seg, group_size)[:, None]
    row_idx = jnp.repeat(my_rows, group_size)[:, None]
    attended = attention(
        q_rot.reshape(rows_mdl * heads_dev, head_dim),
        flat_pages,
        flat_suffix,
        row_prefix,
        row_seg,
        row_idx,
        key_prefix,
        seg_row[None, :],
        scale=score_scale,
    ).reshape(rows_mdl, heads_dev * head_dim)
    partial_out = jnp.dot(
        lax.all_gather(attended, "mdl", axis=0, tiled=True),
        w_out,
        preferred_element_type=jnp.float32,
    )
    out_sum = scatter_sum(partial_out.astype(jnp.bfloat16), "tok").astype(jnp.bfloat16)
    residual = tokens + out_sum.astype(jnp.float32)
    out_all = lax.all_gather(out_sum, "tok", axis=0, tiled=True)
    squares_ffn = lax.psum(jnp.sum(residual * residual, -1), "mdl")
    squares_ffn_all = lax.all_gather(squares_ffn, "tok", axis=0, tiled=True)
    residual_all = hidden_all_f + out_all.astype(jnp.float32)
    ffn_all = (
        residual_all * lax.rsqrt(squares_ffn_all[:, None] / model_width + EPS) * ffn_gain
    ).astype(jnp.bfloat16)
    w_pair = jnp.concatenate([w_gate, w_up], 1)
    ff_dev = w_gate.shape[1]
    partial_ffn = jnp.dot(ffn_all, w_pair, preferred_element_type=jnp.float32)
    summed = lax.psum_scatter(
        partial_ffn.astype(jnp.bfloat16), "mdl", scatter_dimension=0, tiled=True
    ).astype(jnp.float32)
    activated = (jax.nn.silu(summed[:, :ff_dev]) * summed[:, ff_dev:]).astype(jnp.bfloat16)
    partial_down = jnp.dot(
        lax.all_gather(activated, "mdl", axis=0, tiled=True),
        w_down,
        preferred_element_type=jnp.float32,
    )
    final_rows = residual + scatter_sum(partial_down.astype(jnp.bfloat16), "tok")
    tok_start = tok_idx * tok_rows
    my_tok_rows = tok_start + jnp.arange(tok_rows, dtype=jnp.int32)
    tok_seg = lax.dynamic_slice_in_dim(seg_row, tok_start, tok_rows)
    row_squares = jnp.sum(final_rows * final_rows, -1)
    req_squares = jnp.sum(
        jnp.where(tok_seg[:, None] == requests[None, :], row_squares[:, None], 0.0), 0
    )
    ends = offsets + counts - 1
    picked = ends[:, None] == my_tok_rows[None, :]
    last_part = jnp.sum(jnp.where(picked[:, :, None], final_rows[None, :, :], 0.0), 1)
    last_squares = jnp.sum(last_part * last_part, -1)
    packed = jnp.concatenate([last_part, req_squares[:, None], last_squares[:, None]], 1)
    packed = lax.psum(packed, "tok")
    blocks = lax.all_gather(packed, "mdl", axis=0, tiled=False)
    mdl_count = blocks.shape[0]
    last_rows = jnp.transpose(blocks[:, :, :feat_dev], (1, 0, 2)).reshape(req_count, model_width)
    req_total = jnp.sum(blocks[:, :, feat_dev], 0)
    last_total = jnp.sum(blocks[:, :, feat_dev + 1], 0)
    req_norm = jnp.sqrt(req_total / (counts.astype(jnp.float32) * model_width) + EPS)
    last_own = (
        last_rows * lax.rsqrt(last_total[:, None] / model_width + EPS) * final_gain
    ).astype(jnp.bfloat16)
    last_normed = lax.all_gather(last_own, "grp", axis=0, tiled=True)
    logits = lax.dot_general(
        last_normed, lm_head, (((1,), (1,)), ((), ())), preferred_element_type=jnp.float32
    )
    local_max = jnp.max(logits, -1)
    local_max = lax.pmax(local_max, "mdl")
    local_max = lax.pmax(local_max, "tok")
    max_logit = lax.pmax(local_max, "grp").reshape(groups_total, req_count)
    return (
        final_rows.astype(jnp.bfloat16)[None],
        appended[None],
        req_norm[None],
        max_logit,
        logits,
    )


def solution(mesh):
    return jax.shard_map(
        on_device,
        mesh=mesh,
        in_specs=(
            P("grp", "tok", "mdl"),
            P(),
            P(),
            P(),
            P(("grp", "mdl"), None, "tok", None),
            P("mdl"),
            P("mdl", "tok"),
            P("mdl", "tok"),
            P("mdl", "tok"),
            P("tok", "mdl"),
            P("mdl"),
            P("mdl", "tok"),
            P("mdl", "tok"),
            P("tok", "mdl"),
            P(),
            P(("grp", "tok", "mdl"), None),
        ),
        out_specs=(
            P("grp", "tok", "mdl"),
            P("grp", "mdl", "tok", None),
            P("grp", None),
            P(),
            P(None, ("grp", "tok", "mdl")),
        ),
        check_vma=False,
    )
```

```python
import functools

import jax
import jax.numpy as jnp
from jax import lax
from jax.sharding import PartitionSpec as P
from jax.experimental import pallas as pl
from jax.experimental.pallas import tpu as pltpu

PREFIX = 4096
PAGE = 256


EPS = 1e-06
THETA = 1000000.0
NEG = -1e30


def attn_kernel(flags_ref, q_ref, pkv_ref, skv_ref, rp_ref, rs_ref, ri_ref, kp_ref, ks_ref, o_ref, m_ref, t_ref, a_ref, *, scale, head_dim, block_keys):
    i = pl.program_id(0)
    n_pre = pkv_ref.shape[0] // block_keys
    n_suf = skv_ref.shape[0] // block_keys
    m_ref[...] = jnp.full(m_ref.shape, NEG, jnp.float32)
    t_ref[...] = jnp.zeros(t_ref.shape, jnp.float32)
    a_ref[...] = jnp.zeros(a_ref.shape, jnp.float32)

    def update(s, ok, v):
        m_old = m_ref[...]
        m_new = jnp.maximum(m_old, jnp.max(jnp.where(ok, s, NEG), -1, keepdims=True))
        alpha = jnp.exp(m_old - m_new)
        p = jnp.where(ok, jnp.exp(s - m_new), 0.0)
        t_ref[...] = t_ref[...] * alpha + jnp.sum(p, -1, keepdims=True)
        a_ref[...] = a_ref[...] * alpha + jnp.dot(p.astype(jnp.bfloat16), v, preferred_element_type=jnp.float32)
        m_ref[...] = m_new

    def pre_step(b, carry):
        @pl.when(flags_ref[i, b] > 0)
        def _():
            start = pl.multiple_of(b * block_keys, block_keys)
            kv = pkv_ref[pl.ds(start, block_keys), :]
            s = lax.dot_general(q_ref[...], kv[:, :head_dim], (((1,), (1,)), ((), ())), preferred_element_type=jnp.float32) * scale
            ok = rp_ref[...] == kp_ref[:, pl.ds(start, block_keys)]
            update(s, ok, kv[:, head_dim:])
        return carry

    def suf_step(b, carry):
        @pl.when(flags_ref[i, n_pre + b] > 0)
        def _():
            start = pl.multiple_of(b * block_keys, block_keys)
            kv = skv_ref[pl.ds(start, block_keys), :]
            s = lax.dot_general(q_ref[...], kv[:, :head_dim], (((1,), (1,)), ((), ())), preferred_element_type=jnp.float32) * scale
            key_idx = start + lax.broadcasted_iota(jnp.int32, (1, block_keys), 1)
            ok = (rs_ref[...] == ks_ref[:, pl.ds(start, block_keys)]) & (key_idx <= ri_ref[...])
            update(s, ok, kv[:, head_dim:])
        return carry

    lax.fori_loop(0, n_pre, pre_step, 0)
    lax.fori_loop(0, n_suf, suf_step, 0)
    o_ref[...] = (a_ref[...] / t_ref[...]).astype(o_ref.dtype)


def attention(q, pkv, skv, row_prefix, row_seg, row_idx, key_prefix, key_seg, *, scale, block_rows=128, block_keys=256):
    n_rows, head_dim = q.shape
    n_blocks = n_rows // block_rows
    pre_blocks = key_prefix.reshape(-1, block_keys)[:, 0]
    rows_prefix = row_prefix.reshape(n_blocks, block_rows)
    need_pre = jnp.any(rows_prefix[:, :, None] == pre_blocks[None, None, :], 1)
    last_row = jnp.max(row_idx.reshape(n_blocks, block_rows), 1)
    suf_starts = jnp.arange(skv.shape[0] // block_keys, dtype=jnp.int32) * block_keys
    need_suf = suf_starts[None, :] <= last_row[:, None]
    flags = jnp.concatenate([need_pre, need_suf], 1).astype(jnp.int32)
    kern = functools.partial(attn_kernel, scale=scale, head_dim=head_dim, block_keys=block_keys)
    full = lambda shape: pl.BlockSpec(shape, lambda i, f: (0, 0))
    rowb = lambda w: pl.BlockSpec((block_rows, w), lambda i, f: (i, 0))
    return pl.pallas_call(
        kern,
        grid_spec=pltpu.PrefetchScalarGridSpec(
            num_scalar_prefetch=1,
            grid=(n_blocks,),
            in_specs=[rowb(head_dim), full(pkv.shape), full(skv.shape), rowb(1), rowb(1), rowb(1), full(key_prefix.shape), full(key_seg.shape)],
            out_specs=rowb(head_dim),
            scratch_shapes=[pltpu.VMEM((block_rows, 1), jnp.float32), pltpu.VMEM((block_rows, 1), jnp.float32), pltpu.VMEM((block_rows, head_dim), jnp.float32)],
        ),
        out_shape=jax.ShapeDtypeStruct((n_rows, head_dim), jnp.bfloat16),
    )(flags, q, pkv, skv, row_prefix, row_seg, row_idx, key_prefix, key_seg)


def rotate(tensor, positions):
    half_dim = tensor.shape[-1] // 2
    frequency = THETA ** (-(jnp.arange(half_dim, dtype=jnp.float32) * 2.0 / tensor.shape[-1]))
    angles = positions.astype(jnp.float32)[:, None] * frequency[None, :]
    cosine = jnp.cos(angles)[:, None, :]
    sine_part = jnp.sin(angles)[:, None, :]
    first_part = tensor[..., :half_dim]
    second = tensor[..., half_dim:]
    return jnp.concatenate(
        [first_part * cosine - second * sine_part, second * cosine + first_part * sine_part], -1
    )


def scatter_sum(partial, axis):
    count = lax.axis_size(axis)
    pieces = partial.reshape((count, partial.shape[0] // count) + partial.shape[1:])
    pieces = lax.all_to_all(pieces, axis, 0, 0, tiled=False)
    return jnp.sum(pieces.astype(jnp.float32), 0)


def on_device(
    hidden_in,
    seg_ids,
    request_prefix,
    page_table,
    prefix_cache,
    attn_gain,
    w_query,
    w_key,
    w_value,
    w_out,
    ffn_gain,
    w_gate,
    w_up,
    w_down,
    final_gain,
    lm_head,
):
    groups_total = seg_ids.shape[0]
    seq_len = seg_ids.shape[1]
    req_count = request_prefix.shape[1]
    tok_rows = hidden_in.shape[1]
    feat_dev = hidden_in.shape[2]
    model_width = feat_dev * lax.axis_size("mdl")
    head_dim = prefix_cache.shape[3] // 2
    kv_dev = prefix_cache.shape[2]
    heads_dev = w_query.shape[1] // head_dim
    group_size = heads_dev // kv_dev
    page_len = prefix_cache.shape[1]
    slot_total = page_table.shape[0]
    rows_mdl = seq_len // lax.axis_size("mdl")
    group_idx = lax.axis_index("grp")
    tok_idx = lax.axis_index("tok")
    mdl_idx = lax.axis_index("mdl")
    score_scale = head_dim ** (-0.5)
    tokens = hidden_in[0].astype(jnp.float32)
    hidden_all = lax.all_gather(hidden_in[0], "tok", axis=0, tiled=True)
    squares = lax.psum(jnp.sum(tokens * tokens, -1), "mdl")
    squares_all = lax.all_gather(squares, "tok", axis=0, tiled=True)
    hidden_all_f = hidden_all.astype(jnp.float32)
    normed_all = (
        hidden_all_f * lax.rsqrt(squares_all[:, None] / model_width + EPS) * attn_gain
    ).astype(jnp.bfloat16)
    w_joined = jnp.concatenate([w_query, w_key, w_value], 1)
    partial_qkv = jnp.dot(normed_all, w_joined, preferred_element_type=jnp.float32)
    qkv_rows = lax.psum_scatter(partial_qkv, "mdl", scatter_dimension=0, tiled=True)
    q_cols = heads_dev * head_dim
    kv_cols = kv_dev * head_dim
    queries = qkv_rows[:, :q_cols].reshape(rows_mdl, heads_dev, head_dim)
    key_rows = qkv_rows[:, q_cols : q_cols + kv_cols].reshape(rows_mdl, kv_dev, head_dim)
    value_rows = qkv_rows[:, q_cols + kv_cols :].reshape(rows_mdl, kv_dev, head_dim)
    seg_row = lax.dynamic_index_in_dim(seg_ids, group_idx, 0, keepdims=False)
    prefix_row = lax.dynamic_index_in_dim(request_prefix, group_idx, 0, keepdims=False)
    requests = jnp.arange(req_count, dtype=jnp.int32)
    member = seg_row[:, None] == requests[None, :]
    counts = jnp.sum(member.astype(jnp.int32), 0)
    offsets = jnp.cumsum(counts) - counts
    row_start = mdl_idx * rows_mdl
    my_rows = row_start + jnp.arange(rows_mdl, dtype=jnp.int32)
    my_seg = lax.dynamic_slice_in_dim(seg_row, row_start, rows_mdl)
    my_member = my_seg[:, None] == requests[None, :]
    positions = PREFIX + my_rows - jnp.sum(jnp.where(my_member, offsets[None, :], 0), 1)
    my_prefix = jnp.sum(jnp.where(my_member, prefix_row[None, :], 0), 1)
    q_rot = (
        rotate(queries, positions)
        .astype(jnp.bfloat16)
        .reshape(rows_mdl, kv_dev, group_size, head_dim)
    )
    k_rot = rotate(key_rows, positions).astype(jnp.bfloat16)
    appended = jnp.concatenate([k_rot, value_rows.astype(jnp.bfloat16)], -1)
    suffix = lax.all_gather(appended, "mdl", axis=0, tiled=True)
    slot_ids = jnp.arange(slot_total, dtype=jnp.int32)
    pages_each = PREFIX // PAGE
    slot_prefix = jnp.sum(
        jnp.where(page_table[None, :] == slot_ids[:, None], (slot_ids // pages_each)[None, :], 0), 1
    )
    piece = lax.all_gather(prefix_cache, ("grp", "mdl"), axis=0, tiled=True)
    page_count = piece.shape[0]
    key_prefix = jnp.repeat(slot_prefix, page_len)[None, :]
    flat_pages = piece.reshape(page_count * page_len, 2 * head_dim)
    flat_suffix = suffix.reshape(seq_len, 2 * head_dim)
    row_prefix = jnp.repeat(my_prefix, group_size)[:, None]
    row_seg = jnp.repeat(my_seg, group_size)[:, None]
    row_idx = jnp.repeat(my_rows, group_size)[:, None]
    attended = attention(
        q_rot.reshape(rows_mdl * heads_dev, head_dim),
        flat_pages,
        flat_suffix,
        row_prefix,
        row_seg,
        row_idx,
        key_prefix,
        seg_row[None, :],
        scale=score_scale,
    ).reshape(rows_mdl, heads_dev * head_dim)
    partial_out = jnp.dot(
        lax.all_gather(attended, "mdl", axis=0, tiled=True),
        w_out,
        preferred_element_type=jnp.float32,
    )
    out_sum = scatter_sum(partial_out.astype(jnp.bfloat16), "tok").astype(jnp.bfloat16)
    residual = tokens + out_sum.astype(jnp.float32)
    out_all = lax.all_gather(out_sum, "tok", axis=0, tiled=True)
    squares_ffn = lax.psum(jnp.sum(residual * residual, -1), "mdl")
    squares_ffn_all = lax.all_gather(squares_ffn, "tok", axis=0, tiled=True)
    residual_all = hidden_all_f + out_all.astype(jnp.float32)
    ffn_all = (
        residual_all * lax.rsqrt(squares_ffn_all[:, None] / model_width + EPS) * ffn_gain
    ).astype(jnp.bfloat16)
    w_pair = jnp.concatenate([w_gate, w_up], 1)
    ff_dev = w_gate.shape[1]
    partial_ffn = jnp.dot(ffn_all, w_pair, preferred_element_type=jnp.float32)
    summed = lax.psum_scatter(
        partial_ffn.astype(jnp.bfloat16), "mdl", scatter_dimension=0, tiled=True
    ).astype(jnp.float32)
    activated = (jax.nn.silu(summed[:, :ff_dev]) * summed[:, ff_dev:]).astype(jnp.bfloat16)
    partial_down = jnp.dot(
        lax.all_gather(activated, "mdl", axis=0, tiled=True),
        w_down,
        preferred_element_type=jnp.float32,
    )
    final_rows = residual + scatter_sum(partial_down.astype(jnp.bfloat16), "tok")
    tok_start = tok_idx * tok_rows
    my_tok_rows = tok_start + jnp.arange(tok_rows, dtype=jnp.int32)
    tok_seg = lax.dynamic_slice_in_dim(seg_row, tok_start, tok_rows)
    row_squares = jnp.sum(final_rows * final_rows, -1)
    req_squares = jnp.sum(
        jnp.where(tok_seg[:, None] == requests[None, :], row_squares[:, None], 0.0), 0
    )
    ends = offsets + counts - 1
    picked = ends[:, None] == my_tok_rows[None, :]
    last_part = jnp.sum(jnp.where(picked[:, :, None], final_rows[None, :, :], 0.0), 1)
    last_squares = jnp.sum(last_part * last_part, -1)
    packed = jnp.concatenate([last_part, req_squares[:, None], last_squares[:, None]], 1)
    packed = lax.psum(packed, "tok")
    blocks = lax.all_gather(packed, "mdl", axis=0, tiled=False)
    mdl_count = blocks.shape[0]
    last_rows = jnp.transpose(blocks[:, :, :feat_dev], (1, 0, 2)).reshape(req_count, model_width)
    req_total = jnp.sum(blocks[:, :, feat_dev], 0)
    last_total = jnp.sum(blocks[:, :, feat_dev + 1], 0)
    req_norm = jnp.sqrt(req_total / (counts.astype(jnp.float32) * model_width) + EPS)
    last_own = (
        last_rows * lax.rsqrt(last_total[:, None] / model_width + EPS) * final_gain
    ).astype(jnp.bfloat16)
    last_normed = lax.all_gather(last_own, "grp", axis=0, tiled=True)
    logits = lax.dot_general(
        last_normed, lm_head, (((1,), (1,)), ((), ())), preferred_element_type=jnp.float32
    )
    local_max = jnp.max(logits, -1)
    local_max = lax.pmax(local_max, "mdl")
    local_max = lax.pmax(local_max, "tok")
    max_logit = lax.pmax(local_max, "grp").reshape(groups_total, req_count)
    return (
        final_rows.astype(jnp.bfloat16)[None],
        appended[None],
        req_norm[None],
        max_logit,
        logits,
    )


def solution(mesh):
    return jax.shard_map(
        on_device,
        mesh=mesh,
        in_specs=(
            P("grp", "tok", "mdl"),
            P(),
            P(),
            P(),
            P(("grp", "mdl"), None, "tok", None),
            P("mdl"),
            P("mdl", "tok"),
            P("mdl", "tok"),
            P("mdl", "tok"),
            P("tok", "mdl"),
            P("mdl"),
            P("mdl", "tok"),
            P("mdl", "tok"),
            P("tok", "mdl"),
            P(),
            P(("grp", "tok", "mdl"), None),
        ),
        out_specs=(
            P("grp", "tok", "mdl"),
            P("grp", "mdl", "tok", None),
            P("grp", None),
            P(),
            P(None, ("grp", "tok", "mdl")),
        ),
        check_vma=False,
    )
```

```python
import jax
import jax.numpy as jnp
from jax import lax
from jax.sharding import PartitionSpec as P

PREFIX = 4096
PAGE = 256


EPS = 1e-06
THETA = 1000000.0
NEG = -1e30


def rotate(tensor, positions):
    half_dim = tensor.shape[-1] // 2
    frequency = THETA ** (-(jnp.arange(half_dim, dtype=jnp.float32) * 2.0 / tensor.shape[-1]))
    angles = positions.astype(jnp.float32)[:, None] * frequency[None, :]
    cosine = jnp.cos(angles)[:, None, :]
    sine_part = jnp.sin(angles)[:, None, :]
    first_part = tensor[..., :half_dim]
    second = tensor[..., half_dim:]
    return jnp.concatenate(
        [first_part * cosine - second * sine_part, second * cosine + first_part * sine_part], -1
    )


def scatter_sum(partial, axis):
    count = lax.axis_size(axis)
    pieces = partial.reshape((count, partial.shape[0] // count) + partial.shape[1:])
    pieces = lax.all_to_all(pieces, axis, 0, 0, tiled=False)
    return jnp.sum(pieces.astype(jnp.float32), 0)


def on_device(
    hidden_in,
    seg_ids,
    request_prefix,
    page_table,
    prefix_cache,
    attn_gain,
    w_query,
    w_key,
    w_value,
    w_out,
    ffn_gain,
    w_gate,
    w_up,
    w_down,
    final_gain,
    lm_head,
):
    groups_total = seg_ids.shape[0]
    seq_len = seg_ids.shape[1]
    req_count = request_prefix.shape[1]
    tok_rows = hidden_in.shape[1]
    feat_dev = hidden_in.shape[2]
    model_width = feat_dev * lax.axis_size("mdl")
    head_dim = prefix_cache.shape[3] // 2
    kv_dev = prefix_cache.shape[2]
    heads_dev = w_query.shape[1] // head_dim
    group_size = heads_dev // kv_dev
    page_len = prefix_cache.shape[1]
    slot_total = page_table.shape[0]
    rows_mdl = seq_len // lax.axis_size("mdl")
    group_idx = lax.axis_index("grp")
    tok_idx = lax.axis_index("tok")
    mdl_idx = lax.axis_index("mdl")
    score_scale = head_dim ** (-0.5)
    tokens = hidden_in[0].astype(jnp.float32)
    hidden_all = lax.all_gather(hidden_in[0], "tok", axis=0, tiled=True)
    squares = lax.psum(jnp.sum(tokens * tokens, -1), "mdl")
    squares_all = lax.all_gather(squares, "tok", axis=0, tiled=True)
    hidden_all_f = hidden_all.astype(jnp.float32)
    normed_all = (
        hidden_all_f * lax.rsqrt(squares_all[:, None] / model_width + EPS) * attn_gain
    ).astype(jnp.bfloat16)
    w_joined = jnp.concatenate([w_query, w_key, w_value], 1)
    partial_qkv = jnp.dot(normed_all, w_joined, preferred_element_type=jnp.float32)
    qkv_rows = lax.psum_scatter(partial_qkv, "mdl", scatter_dimension=0, tiled=True)
    q_cols = heads_dev * head_dim
    kv_cols = kv_dev * head_dim
    queries = qkv_rows[:, :q_cols].reshape(rows_mdl, heads_dev, head_dim)
    key_rows = qkv_rows[:, q_cols : q_cols + kv_cols].reshape(rows_mdl, kv_dev, head_dim)
    value_rows = qkv_rows[:, q_cols + kv_cols :].reshape(rows_mdl, kv_dev, head_dim)
    seg_row = lax.dynamic_index_in_dim(seg_ids, group_idx, 0, keepdims=False)
    prefix_row = lax.dynamic_index_in_dim(request_prefix, group_idx, 0, keepdims=False)
    requests = jnp.arange(req_count, dtype=jnp.int32)
    member = seg_row[:, None] == requests[None, :]
    counts = jnp.sum(member.astype(jnp.int32), 0)
    offsets = jnp.cumsum(counts) - counts
    row_start = mdl_idx * rows_mdl
    my_rows = row_start + jnp.arange(rows_mdl, dtype=jnp.int32)
    my_seg = lax.dynamic_slice_in_dim(seg_row, row_start, rows_mdl)
    my_member = my_seg[:, None] == requests[None, :]
    positions = PREFIX + my_rows - jnp.sum(jnp.where(my_member, offsets[None, :], 0), 1)
    my_prefix = jnp.sum(jnp.where(my_member, prefix_row[None, :], 0), 1)
    q_rot = (
        rotate(queries, positions)
        .astype(jnp.bfloat16)
        .reshape(rows_mdl, kv_dev, group_size, head_dim)
    )
    k_rot = rotate(key_rows, positions).astype(jnp.bfloat16)
    appended = jnp.concatenate([k_rot, value_rows.astype(jnp.bfloat16)], -1)
    suffix = lax.all_gather(appended, "mdl", axis=0, tiled=True)
    every_row = jnp.arange(seq_len, dtype=jnp.int32)
    suffix_ok = ((seg_row[None, :] == my_seg[:, None]) & (every_row[None, :] <= my_rows[:, None]))[
        :, None, None, :
    ]
    suffix_scores = (
        jnp.einsum(
            "rcgd,tcd->rcgt", q_rot, suffix[..., :head_dim], preferred_element_type=jnp.float32
        )
        * score_scale
    )
    suffix_scores = jnp.where(suffix_ok, suffix_scores, NEG)
    row_max = jnp.max(suffix_scores, -1)
    suffix_weights = jnp.where(suffix_ok, jnp.exp(suffix_scores - row_max[..., None]), 0.0)
    row_total = jnp.sum(suffix_weights, -1)
    mixed = jnp.einsum(
        "rcgt,tcd->rcgd",
        suffix_weights.astype(jnp.bfloat16),
        suffix[..., head_dim:],
        preferred_element_type=jnp.float32,
    )
    slot_ids = jnp.arange(slot_total, dtype=jnp.int32)
    pages_each = PREFIX // PAGE
    slot_prefix = jnp.sum(
        jnp.where(page_table[None, :] == slot_ids[:, None], (slot_ids // pages_each)[None, :], 0), 1
    )
    piece = lax.all_gather(prefix_cache, ("grp", "mdl"), axis=0, tiled=True)
    page_count = piece.shape[0]
    key_prefix = jnp.repeat(slot_prefix, page_len)
    allowed = (my_prefix[:, None] == key_prefix[None, :])[:, None, None, :]
    flat_pages = piece.reshape(page_count * page_len, kv_dev, 2 * head_dim)
    scores = (
        jnp.einsum(
            "rcgd,kcd->rcgk", q_rot, flat_pages[..., :head_dim], preferred_element_type=jnp.float32
        )
        * score_scale
    )
    scores = jnp.where(allowed, scores, NEG)
    new_max = jnp.maximum(row_max, jnp.max(scores, -1))
    factor = jnp.exp(row_max - new_max)
    page_weights = jnp.where(allowed, jnp.exp(scores - new_max[..., None]), 0.0)
    new_total = row_total * factor + jnp.sum(page_weights, -1)
    new_mixed = mixed * factor[..., None] + jnp.einsum(
        "rcgk,kcd->rcgd",
        page_weights.astype(jnp.bfloat16),
        flat_pages[..., head_dim:],
        preferred_element_type=jnp.float32,
    )
    attended = (
        (new_mixed / new_total[..., None])
        .astype(jnp.bfloat16)
        .reshape(rows_mdl, heads_dev * head_dim)
    )
    partial_out = jnp.dot(
        lax.all_gather(attended, "mdl", axis=0, tiled=True),
        w_out,
        preferred_element_type=jnp.float32,
    )
    out_sum = scatter_sum(partial_out.astype(jnp.bfloat16), "tok").astype(jnp.bfloat16)
    residual = tokens + out_sum.astype(jnp.float32)
    out_all = lax.all_gather(out_sum, "tok", axis=0, tiled=True)
    squares_ffn = lax.psum(jnp.sum(residual * residual, -1), "mdl")
    squares_ffn_all = lax.all_gather(squares_ffn, "tok", axis=0, tiled=True)
    residual_all = hidden_all_f + out_all.astype(jnp.float32)
    ffn_all = (
        residual_all * lax.rsqrt(squares_ffn_all[:, None] / model_width + EPS) * ffn_gain
    ).astype(jnp.bfloat16)
    w_pair = jnp.concatenate([w_gate, w_up], 1)
    ff_dev = w_gate.shape[1]
    partial_ffn = jnp.dot(ffn_all, w_pair, preferred_element_type=jnp.float32)
    summed = lax.psum_scatter(
        partial_ffn.astype(jnp.bfloat16), "mdl", scatter_dimension=0, tiled=True
    ).astype(jnp.float32)
    activated = (jax.nn.silu(summed[:, :ff_dev]) * summed[:, ff_dev:]).astype(jnp.bfloat16)
    partial_down = jnp.dot(
        lax.all_gather(activated, "mdl", axis=0, tiled=True),
        w_down,
        preferred_element_type=jnp.float32,
    )
    down_sum = lax.psum_scatter(
        partial_down.astype(jnp.bfloat16), "tok", scatter_dimension=0, tiled=True
    )
    final_rows = residual + down_sum.astype(jnp.float32)
    tok_start = tok_idx * tok_rows
    my_tok_rows = tok_start + jnp.arange(tok_rows, dtype=jnp.int32)
    tok_seg = lax.dynamic_slice_in_dim(seg_row, tok_start, tok_rows)
    row_squares = jnp.sum(final_rows * final_rows, -1)
    req_squares = jnp.sum(
        jnp.where(tok_seg[:, None] == requests[None, :], row_squares[:, None], 0.0), 0
    )
    ends = offsets + counts - 1
    picked = ends[:, None] == my_tok_rows[None, :]
    last_res = jnp.sum(jnp.where(picked[:, :, None], residual[None, :, :], 0.0), 1)
    last_down = jnp.take(partial_down, ends, axis=0, mode="clip")
    last_part = lax.psum(last_res + last_down, "tok")
    last_squares = jnp.sum(last_part * last_part, -1)
    packed = jnp.concatenate([last_part, last_squares[:, None]], 1)
    blocks = lax.all_gather(packed, "mdl", axis=0, tiled=False)
    last_rows = jnp.transpose(blocks[:, :, :feat_dev], (1, 0, 2)).reshape(req_count, model_width)
    last_total = jnp.sum(blocks[:, :, feat_dev], 0)
    req_squares, _ = lax.optimization_barrier((req_squares, last_part))
    req_total = lax.psum(lax.psum(req_squares, "tok"), "mdl")
    req_norm = jnp.sqrt(req_total / (counts.astype(jnp.float32) * model_width) + EPS)
    last_own = (
        last_rows * lax.rsqrt(last_total[:, None] / model_width + EPS) * final_gain
    ).astype(jnp.bfloat16)
    last_normed = lax.all_gather(last_own, "grp", axis=0, tiled=True)
    logits = lax.dot_general(
        last_normed, lm_head, (((1,), (1,)), ((), ())), preferred_element_type=jnp.float32
    )
    local_max = jnp.max(logits, -1)
    local_max = lax.pmax(local_max, "mdl")
    local_max = lax.pmax(local_max, "tok")
    max_logit = lax.pmax(local_max, "grp").reshape(groups_total, req_count)
    return (
        final_rows.astype(jnp.bfloat16)[None],
        appended[None],
        req_norm[None],
        max_logit,
        logits,
    )


def solution(mesh):
    return jax.shard_map(
        on_device,
        mesh=mesh,
        in_specs=(
            P("grp", "tok", "mdl"),
            P(),
            P(),
            P(),
            P(("grp", "mdl"), None, "tok", None),
            P("mdl"),
            P("mdl", "tok"),
            P("mdl", "tok"),
            P("mdl", "tok"),
            P("tok", "mdl"),
            P("mdl"),
            P("mdl", "tok"),
            P("mdl", "tok"),
            P("tok", "mdl"),
            P(),
            P(("grp", "tok", "mdl"), None),
        ),
        out_specs=(
            P("grp", "tok", "mdl"),
            P("grp", "mdl", "tok", None),
            P("grp", None),
            P(),
            P(None, ("grp", "tok", "mdl")),
        ),
        check_vma=False,
    )
```

```python
import jax
import jax.numpy as jnp
from jax import lax
from jax.sharding import PartitionSpec as P

PREFIX = 4096
PAGE = 256


EPS = 1e-06
THETA = 1000000.0
NEG = -1e30


def rotate(tensor, positions):
    half_dim = tensor.shape[-1] // 2
    frequency = THETA ** (-(jnp.arange(half_dim, dtype=jnp.float32) * 2.0 / tensor.shape[-1]))
    angles = positions.astype(jnp.float32)[:, None] * frequency[None, :]
    cosine = jnp.cos(angles)[:, None, :]
    sine_part = jnp.sin(angles)[:, None, :]
    first_part = tensor[..., :half_dim]
    second = tensor[..., half_dim:]
    return jnp.concatenate(
        [first_part * cosine - second * sine_part, second * cosine + first_part * sine_part], -1
    )


def scatter_sum(partial, axis):
    count = lax.axis_size(axis)
    pieces = partial.reshape((count, partial.shape[0] // count) + partial.shape[1:])
    pieces = lax.all_to_all(pieces, axis, 0, 0, tiled=False)
    return jnp.sum(pieces.astype(jnp.float32), 0)


def on_device(
    hidden_in,
    seg_ids,
    request_prefix,
    page_table,
    prefix_cache,
    attn_gain,
    w_query,
    w_key,
    w_value,
    w_out,
    ffn_gain,
    w_gate,
    w_up,
    w_down,
    final_gain,
    lm_head,
):
    groups_total = seg_ids.shape[0]
    seq_len = seg_ids.shape[1]
    req_count = request_prefix.shape[1]
    tok_rows = hidden_in.shape[1]
    feat_dev = hidden_in.shape[2]
    model_width = feat_dev * lax.axis_size("mdl")
    head_dim = prefix_cache.shape[3] // 2
    kv_dev = prefix_cache.shape[2]
    heads_dev = w_query.shape[1] // head_dim
    group_size = heads_dev // kv_dev
    page_len = prefix_cache.shape[1]
    slot_total = page_table.shape[0]
    rows_mdl = seq_len // lax.axis_size("mdl")
    group_idx = lax.axis_index("grp")
    tok_idx = lax.axis_index("tok")
    mdl_idx = lax.axis_index("mdl")
    score_scale = head_dim ** (-0.5)
    tokens = hidden_in[0].astype(jnp.float32)
    hidden_all = lax.all_gather(hidden_in[0], "tok", axis=0, tiled=True)
    squares = lax.psum(jnp.sum(tokens * tokens, -1), "mdl")
    squares_all = lax.all_gather(squares, "tok", axis=0, tiled=True)
    hidden_all_f = hidden_all.astype(jnp.float32)
    normed_all = (
        hidden_all_f * lax.rsqrt(squares_all[:, None] / model_width + EPS) * attn_gain
    ).astype(jnp.bfloat16)
    w_joined = jnp.concatenate([w_query, w_key, w_value], 1)
    partial_qkv = jnp.dot(normed_all, w_joined, preferred_element_type=jnp.float32)
    qkv_rows = lax.psum_scatter(partial_qkv, "mdl", scatter_dimension=0, tiled=True)
    q_cols = heads_dev * head_dim
    kv_cols = kv_dev * head_dim
    queries = qkv_rows[:, :q_cols].reshape(rows_mdl, heads_dev, head_dim)
    key_rows = qkv_rows[:, q_cols : q_cols + kv_cols].reshape(rows_mdl, kv_dev, head_dim)
    value_rows = qkv_rows[:, q_cols + kv_cols :].reshape(rows_mdl, kv_dev, head_dim)
    seg_row = lax.dynamic_index_in_dim(seg_ids, group_idx, 0, keepdims=False)
    prefix_row = lax.dynamic_index_in_dim(request_prefix, group_idx, 0, keepdims=False)
    requests = jnp.arange(req_count, dtype=jnp.int32)
    member = seg_row[:, None] == requests[None, :]
    counts = jnp.sum(member.astype(jnp.int32), 0)
    offsets = jnp.cumsum(counts) - counts
    row_start = mdl_idx * rows_mdl
    my_rows = row_start + jnp.arange(rows_mdl, dtype=jnp.int32)
    my_seg = lax.dynamic_slice_in_dim(seg_row, row_start, rows_mdl)
    my_member = my_seg[:, None] == requests[None, :]
    positions = PREFIX + my_rows - jnp.sum(jnp.where(my_member, offsets[None, :], 0), 1)
    my_prefix = jnp.sum(jnp.where(my_member, prefix_row[None, :], 0), 1)
    q_rot = (
        rotate(queries, positions)
        .astype(jnp.bfloat16)
        .reshape(rows_mdl, kv_dev, group_size, head_dim)
    )
    k_rot = rotate(key_rows, positions).astype(jnp.bfloat16)
    appended = jnp.concatenate([k_rot, value_rows.astype(jnp.bfloat16)], -1)
    suffix = lax.all_gather(appended, "mdl", axis=0, tiled=True)
    every_row = jnp.arange(seq_len, dtype=jnp.int32)
    suffix_ok = ((seg_row[None, :] == my_seg[:, None]) & (every_row[None, :] <= my_rows[:, None]))[
        :, None, None, :
    ]
    suffix_scores = (
        jnp.einsum(
            "rcgd,tcd->rcgt", q_rot, suffix[..., :head_dim], preferred_element_type=jnp.float32
        )
        * score_scale
    )
    suffix_scores = jnp.where(suffix_ok, suffix_scores, NEG)
    row_max = jnp.max(suffix_scores, -1)
    suffix_weights = jnp.where(suffix_ok, jnp.exp(suffix_scores - row_max[..., None]), 0.0)
    row_total = jnp.sum(suffix_weights, -1)
    mixed = jnp.einsum(
        "rcgt,tcd->rcgd",
        suffix_weights.astype(jnp.bfloat16),
        suffix[..., head_dim:],
        preferred_element_type=jnp.float32,
    )
    slot_ids = jnp.arange(slot_total, dtype=jnp.int32)
    pages_each = PREFIX // PAGE
    slot_prefix = jnp.sum(
        jnp.where(page_table[None, :] == slot_ids[:, None], (slot_ids // pages_each)[None, :], 0), 1
    )
    piece = lax.all_gather(prefix_cache, ("grp", "mdl"), axis=0, tiled=True)
    page_count = piece.shape[0]
    key_prefix = jnp.repeat(slot_prefix, page_len)
    allowed = (my_prefix[:, None] == key_prefix[None, :])[:, None, None, :]
    flat_pages = piece.reshape(page_count * page_len, kv_dev, 2 * head_dim)
    scores = (
        jnp.einsum(
            "rcgd,kcd->rcgk", q_rot, flat_pages[..., :head_dim], preferred_element_type=jnp.float32
        )
        * score_scale
    )
    scores = jnp.where(allowed, scores, NEG)
    new_max = jnp.maximum(row_max, jnp.max(scores, -1))
    factor = jnp.exp(row_max - new_max)
    page_weights = jnp.where(allowed, jnp.exp(scores - new_max[..., None]), 0.0)
    new_total = row_total * factor + jnp.sum(page_weights, -1)
    new_mixed = mixed * factor[..., None] + jnp.einsum(
        "rcgk,kcd->rcgd",
        page_weights.astype(jnp.bfloat16),
        flat_pages[..., head_dim:],
        preferred_element_type=jnp.float32,
    )
    attended = (
        (new_mixed / new_total[..., None])
        .astype(jnp.bfloat16)
        .reshape(rows_mdl, heads_dev * head_dim)
    )
    partial_out = jnp.dot(
        lax.all_gather(attended, "mdl", axis=0, tiled=True),
        w_out,
        preferred_element_type=jnp.float32,
    )
    out_sum = scatter_sum(partial_out.astype(jnp.bfloat16), "tok").astype(jnp.bfloat16)
    residual = tokens + out_sum.astype(jnp.float32)
    out_all = lax.all_gather(out_sum, "tok", axis=0, tiled=True)
    squares_ffn = lax.psum(jnp.sum(residual * residual, -1), "mdl")
    squares_ffn_all = lax.all_gather(squares_ffn, "tok", axis=0, tiled=True)
    residual_all = hidden_all_f + out_all.astype(jnp.float32)
    ffn_all = (
        residual_all * lax.rsqrt(squares_ffn_all[:, None] / model_width + EPS) * ffn_gain
    ).astype(jnp.bfloat16)
    w_pair = jnp.concatenate([w_gate, w_up], 1)
    ff_dev = w_gate.shape[1]
    partial_ffn = jnp.dot(ffn_all, w_pair, preferred_element_type=jnp.float32)
    summed = lax.psum_scatter(
        partial_ffn.astype(jnp.bfloat16), "mdl", scatter_dimension=0, tiled=True
    ).astype(jnp.float32)
    activated = (jax.nn.silu(summed[:, :ff_dev]) * summed[:, ff_dev:]).astype(jnp.bfloat16)
    partial_down = jnp.dot(
        lax.all_gather(activated, "mdl", axis=0, tiled=True),
        w_down,
        preferred_element_type=jnp.float32,
    )
    down_sum = lax.psum_scatter(
        partial_down.astype(jnp.bfloat16), "tok", scatter_dimension=0, tiled=True
    )
    final_rows = residual + down_sum.astype(jnp.float32)
    tok_start = tok_idx * tok_rows
    my_tok_rows = tok_start + jnp.arange(tok_rows, dtype=jnp.int32)
    tok_seg = lax.dynamic_slice_in_dim(seg_row, tok_start, tok_rows)
    row_squares = jnp.sum(final_rows * final_rows, -1)
    req_squares = jnp.sum(
        jnp.where(tok_seg[:, None] == requests[None, :], row_squares[:, None], 0.0), 0
    )
    ends = offsets + counts - 1
    picked = ends[:, None] == my_tok_rows[None, :]
    last_res = jnp.sum(jnp.where(picked[:, :, None], residual[None, :, :], 0.0), 1)
    last_down = jnp.take(partial_down, ends, axis=0, mode="clip")
    last_part = jnp.sum(lax.all_gather(last_res + last_down, "tok", axis=0, tiled=False), 0)
    last_squares = jnp.sum(last_part * last_part, -1)
    packed = jnp.concatenate([last_part, last_squares[:, None]], 1)
    blocks = lax.all_gather(packed, "mdl", axis=0, tiled=False)
    last_rows = jnp.transpose(blocks[:, :, :feat_dev], (1, 0, 2)).reshape(req_count, model_width)
    last_total = jnp.sum(blocks[:, :, feat_dev], 0)
    last_own = (
        last_rows * lax.rsqrt(last_total[:, None] / model_width + EPS) * final_gain
    ).astype(jnp.bfloat16)
    last_normed = lax.all_gather(last_own, "grp", axis=0, tiled=True)
    logits = lax.dot_general(
        last_normed, lm_head, (((1,), (1,)), ((), ())), preferred_element_type=jnp.float32
    )
    local_max = jnp.max(logits, -1)
    rows_total = local_max.shape[0]
    stats = jnp.concatenate([local_max, req_squares])
    stats = lax.all_gather(stats, "tok", axis=0, tiled=False)
    stats = jnp.concatenate([jnp.max(stats[:, :rows_total], 0), jnp.sum(stats[:, rows_total:], 0)])
    stats = lax.all_gather(stats, "mdl", axis=0, tiled=False)
    req_total = jnp.sum(stats[:, rows_total:], 0)
    req_norm = jnp.sqrt(req_total / (counts.astype(jnp.float32) * model_width) + EPS)
    max_logit = lax.pmax(jnp.max(stats[:, :rows_total], 0), "grp").reshape(groups_total, req_count)
    return (
        final_rows.astype(jnp.bfloat16)[None],
        appended[None],
        req_norm[None],
        max_logit,
        logits,
    )


def solution(mesh):
    return jax.shard_map(
        on_device,
        mesh=mesh,
        in_specs=(
            P("grp", "tok", "mdl"),
            P(),
            P(),
            P(),
            P(("grp", "mdl"), None, "tok", None),
            P("mdl"),
            P("mdl", "tok"),
            P("mdl", "tok"),
            P("mdl", "tok"),
            P("tok", "mdl"),
            P("mdl"),
            P("mdl", "tok"),
            P("mdl", "tok"),
            P("tok", "mdl"),
            P(),
            P(("grp", "tok", "mdl"), None),
        ),
        out_specs=(
            P("grp", "tok", "mdl"),
            P("grp", "mdl", "tok", None),
            P("grp", None),
            P(),
            P(None, ("grp", "tok", "mdl")),
        ),
        check_vma=False,
    )
```

```python
import jax
import jax.numpy as jnp
from jax import lax
from jax.sharding import PartitionSpec as P

PREFIX = 4096
PAGE = 256


EPS = 1e-06
THETA = 1000000.0
NEG = -1e30


def rotate(tensor, positions):
    half_dim = tensor.shape[-1] // 2
    frequency = THETA ** (-(jnp.arange(half_dim, dtype=jnp.float32) * 2.0 / tensor.shape[-1]))
    angles = positions.astype(jnp.float32)[:, None] * frequency[None, :]
    cosine = jnp.cos(angles)[:, None, :]
    sine_part = jnp.sin(angles)[:, None, :]
    first_part = tensor[..., :half_dim]
    second = tensor[..., half_dim:]
    return jnp.concatenate(
        [first_part * cosine - second * sine_part, second * cosine + first_part * sine_part], -1
    )


def scatter_sum(partial, axis):
    count = lax.axis_size(axis)
    pieces = partial.reshape((count, partial.shape[0] // count) + partial.shape[1:])
    pieces = lax.all_to_all(pieces, axis, 0, 0, tiled=False)
    return jnp.sum(pieces.astype(jnp.float32), 0)


def on_device(
    hidden_in,
    seg_ids,
    request_prefix,
    page_table,
    prefix_cache,
    attn_gain,
    w_query,
    w_key,
    w_value,
    w_out,
    ffn_gain,
    w_gate,
    w_up,
    w_down,
    final_gain,
    lm_head,
):
    groups_total = seg_ids.shape[0]
    seq_len = seg_ids.shape[1]
    req_count = request_prefix.shape[1]
    tok_rows = hidden_in.shape[1]
    feat_dev = hidden_in.shape[2]
    model_width = feat_dev * lax.axis_size("mdl")
    head_dim = prefix_cache.shape[3] // 2
    kv_dev = prefix_cache.shape[2]
    heads_dev = w_query.shape[1] // head_dim
    group_size = heads_dev // kv_dev
    page_len = prefix_cache.shape[1]
    slot_total = page_table.shape[0]
    rows_mdl = seq_len // lax.axis_size("mdl")
    group_idx = lax.axis_index("grp")
    tok_idx = lax.axis_index("tok")
    mdl_idx = lax.axis_index("mdl")
    score_scale = head_dim ** (-0.5)
    tokens = hidden_in[0].astype(jnp.float32)
    hidden_all = lax.all_gather(hidden_in[0], "tok", axis=0, tiled=True)
    squares = lax.psum(jnp.sum(tokens * tokens, -1), "mdl")
    squares_all = lax.all_gather(squares, "tok", axis=0, tiled=True)
    hidden_all_f = hidden_all.astype(jnp.float32)
    normed_all = (
        hidden_all_f * lax.rsqrt(squares_all[:, None] / model_width + EPS) * attn_gain
    ).astype(jnp.bfloat16)
    w_joined = jnp.concatenate([w_query, w_key, w_value], 1)
    partial_qkv = jnp.dot(normed_all, w_joined, preferred_element_type=jnp.float32)
    qkv_rows = lax.psum_scatter(partial_qkv, "mdl", scatter_dimension=0, tiled=True)
    q_cols = heads_dev * head_dim
    kv_cols = kv_dev * head_dim
    queries = qkv_rows[:, :q_cols].reshape(rows_mdl, heads_dev, head_dim)
    key_rows = qkv_rows[:, q_cols : q_cols + kv_cols].reshape(rows_mdl, kv_dev, head_dim)
    value_rows = qkv_rows[:, q_cols + kv_cols :].reshape(rows_mdl, kv_dev, head_dim)
    seg_row = lax.dynamic_index_in_dim(seg_ids, group_idx, 0, keepdims=False)
    prefix_row = lax.dynamic_index_in_dim(request_prefix, group_idx, 0, keepdims=False)
    requests = jnp.arange(req_count, dtype=jnp.int32)
    member = seg_row[:, None] == requests[None, :]
    counts = jnp.sum(member.astype(jnp.int32), 0)
    offsets = jnp.cumsum(counts) - counts
    row_start = mdl_idx * rows_mdl
    my_rows = row_start + jnp.arange(rows_mdl, dtype=jnp.int32)
    my_seg = lax.dynamic_slice_in_dim(seg_row, row_start, rows_mdl)
    my_member = my_seg[:, None] == requests[None, :]
    positions = PREFIX + my_rows - jnp.sum(jnp.where(my_member, offsets[None, :], 0), 1)
    my_prefix = jnp.sum(jnp.where(my_member, prefix_row[None, :], 0), 1)
    q_rot = (
        rotate(queries, positions)
        .astype(jnp.bfloat16)
        .reshape(rows_mdl, kv_dev, group_size, head_dim)
    )
    k_rot = rotate(key_rows, positions).astype(jnp.bfloat16)
    appended = jnp.concatenate([k_rot, value_rows.astype(jnp.bfloat16)], -1)
    suffix = lax.all_gather(appended, "mdl", axis=0, tiled=True)
    every_row = jnp.arange(seq_len, dtype=jnp.int32)
    suffix_ok = ((seg_row[None, :] == my_seg[:, None]) & (every_row[None, :] <= my_rows[:, None]))[
        :, None, None, :
    ]
    suffix_scores = (
        jnp.einsum(
            "rcgd,tcd->rcgt", q_rot, suffix[..., :head_dim], preferred_element_type=jnp.float32
        )
        * score_scale
    )
    suffix_scores = jnp.where(suffix_ok, suffix_scores, NEG)
    row_max = jnp.max(suffix_scores, -1)
    suffix_weights = jnp.where(suffix_ok, jnp.exp(suffix_scores - row_max[..., None]), 0.0)
    row_total = jnp.sum(suffix_weights, -1)
    mixed = jnp.einsum(
        "rcgt,tcd->rcgd",
        suffix_weights.astype(jnp.bfloat16),
        suffix[..., head_dim:],
        preferred_element_type=jnp.float32,
    )
    slot_ids = jnp.arange(slot_total, dtype=jnp.int32)
    pages_each = PREFIX // PAGE
    slot_prefix = jnp.sum(
        jnp.where(page_table[None, :] == slot_ids[:, None], (slot_ids // pages_each)[None, :], 0), 1
    )
    piece = lax.all_gather(prefix_cache, ("grp", "mdl"), axis=0, tiled=True)
    page_count = piece.shape[0]
    key_prefix = jnp.repeat(slot_prefix, page_len)
    allowed = (my_prefix[:, None] == key_prefix[None, :])[:, None, None, :]
    flat_pages = piece.reshape(page_count * page_len, kv_dev, 2 * head_dim)
    scores = (
        jnp.einsum(
            "rcgd,kcd->rcgk", q_rot, flat_pages[..., :head_dim], preferred_element_type=jnp.float32
        )
        * score_scale
    )
    scores = jnp.where(allowed, scores, NEG)
    new_max = jnp.maximum(row_max, jnp.max(scores, -1))
    factor = jnp.exp(row_max - new_max)
    page_weights = jnp.where(allowed, jnp.exp(scores - new_max[..., None]), 0.0)
    new_total = row_total * factor + jnp.sum(page_weights, -1)
    new_mixed = mixed * factor[..., None] + jnp.einsum(
        "rcgk,kcd->rcgd",
        page_weights.astype(jnp.bfloat16),
        flat_pages[..., head_dim:],
        preferred_element_type=jnp.float32,
    )
    attended = (
        (new_mixed / new_total[..., None])
        .astype(jnp.bfloat16)
        .reshape(rows_mdl, heads_dev * head_dim)
    )
    partial_out = jnp.dot(
        lax.all_gather(attended, "mdl", axis=0, tiled=True),
        w_out,
        preferred_element_type=jnp.float32,
    )
    out_sum = scatter_sum(partial_out.astype(jnp.bfloat16), "tok").astype(jnp.bfloat16)
    residual = tokens + out_sum.astype(jnp.float32)
    out_all = lax.all_gather(out_sum, "tok", axis=0, tiled=True)
    squares_ffn = lax.psum(jnp.sum(residual * residual, -1), "mdl")
    squares_ffn_all = lax.all_gather(squares_ffn, "tok", axis=0, tiled=True)
    residual_all = hidden_all_f + out_all.astype(jnp.float32)
    ffn_all = (
        residual_all * lax.rsqrt(squares_ffn_all[:, None] / model_width + EPS) * ffn_gain
    ).astype(jnp.bfloat16)
    w_pair = jnp.concatenate([w_gate, w_up], 1)
    ff_dev = w_gate.shape[1]
    partial_ffn = jnp.dot(ffn_all, w_pair, preferred_element_type=jnp.float32)
    summed = lax.psum_scatter(
        partial_ffn.astype(jnp.bfloat16), "mdl", scatter_dimension=0, tiled=True
    ).astype(jnp.float32)
    activated = (jax.nn.silu(summed[:, :ff_dev]) * summed[:, ff_dev:]).astype(jnp.bfloat16)
    partial_down = jnp.dot(
        lax.all_gather(activated, "mdl", axis=0, tiled=True),
        w_down,
        preferred_element_type=jnp.float32,
    )
    down_sum = lax.psum_scatter(
        partial_down.astype(jnp.bfloat16), "tok", scatter_dimension=0, tiled=True
    )
    final_rows = residual + down_sum.astype(jnp.float32)
    tok_start = tok_idx * tok_rows
    my_tok_rows = tok_start + jnp.arange(tok_rows, dtype=jnp.int32)
    tok_seg = lax.dynamic_slice_in_dim(seg_row, tok_start, tok_rows)
    row_squares = jnp.sum(final_rows * final_rows, -1)
    req_squares = jnp.sum(
        jnp.where(tok_seg[:, None] == requests[None, :], row_squares[:, None], 0.0), 0
    )
    ends = offsets + counts - 1
    picked = ends[:, None] == my_tok_rows[None, :]
    last_res = jnp.sum(jnp.where(picked[:, :, None], residual[None, :, :], 0.0), 1)
    last_down = jnp.take(partial_down, ends, axis=0, mode="clip")
    by_mdl = lax.all_gather(last_res + last_down, "mdl", axis=0, tiled=False)
    wide = jnp.transpose(by_mdl, (1, 0, 2)).reshape(req_count, model_width)
    last_rows = jnp.sum(lax.all_gather(wide, "tok", axis=0, tiled=False), 0)
    last_total = jnp.sum(last_rows * last_rows, -1)
    last_own = (
        last_rows * lax.rsqrt(last_total[:, None] / model_width + EPS) * final_gain
    ).astype(jnp.bfloat16)
    last_normed = lax.all_gather(last_own, "grp", axis=0, tiled=True)
    logits = lax.dot_general(
        last_normed, lm_head, (((1,), (1,)), ((), ())), preferred_element_type=jnp.float32
    )
    local_max = jnp.max(logits, -1)
    rows_total = local_max.shape[0]
    stats = jnp.concatenate([local_max, req_squares])
    stats = lax.all_gather(stats, "tok", axis=0, tiled=False)
    stats = jnp.concatenate([jnp.max(stats[:, :rows_total], 0), jnp.sum(stats[:, rows_total:], 0)])
    stats = lax.all_gather(stats, "mdl", axis=0, tiled=False)
    req_total = jnp.sum(stats[:, rows_total:], 0)
    req_norm = jnp.sqrt(req_total / (counts.astype(jnp.float32) * model_width) + EPS)
    max_logit = lax.pmax(jnp.max(stats[:, :rows_total], 0), "grp").reshape(groups_total, req_count)
    return (
        final_rows.astype(jnp.bfloat16)[None],
        appended[None],
        req_norm[None],
        max_logit,
        logits,
    )


def solution(mesh):
    return jax.shard_map(
        on_device,
        mesh=mesh,
        in_specs=(
            P("grp", "tok", "mdl"),
            P(),
            P(),
            P(),
            P(("grp", "mdl"), None, "tok", None),
            P("mdl"),
            P("mdl", "tok"),
            P("mdl", "tok"),
            P("mdl", "tok"),
            P("tok", "mdl"),
            P("mdl"),
            P("mdl", "tok"),
            P("mdl", "tok"),
            P("tok", "mdl"),
            P(),
            P(("grp", "tok", "mdl"), None),
        ),
        out_specs=(
            P("grp", "tok", "mdl"),
            P("grp", "mdl", "tok", None),
            P("grp", None),
            P(),
            P(None, ("grp", "tok", "mdl")),
        ),
        check_vma=False,
    )
```
